128 devices in a mesh: kz: 4 (over x_hi, core), en: 32 (over z, y, x_lo).
Axes of the slice: x: 4 (x_hi: 2, x_lo: 2; x = x_hi * 2 + x_lo), y: 4, z: 4, core: 2. Of those that a mesh axis runs over, the one named last changes fastest.
Arguments:
- sigma_less: bfloat16 [4, 128, 3, 2, 128, 128], P('kz', 'en'), as said below
- sigma_great: bfloat16 [4, 128, 3, 2, 128, 128], P('kz', 'en'), as said below
- onsite_table: float32 [3, 128, 128], replicated, as said below
- cos_coupling: float32 [3, 128, 128], replicated, as said below
- slab_coupling: float32 [2, 128, 128], replicated, may hold values from -0.25 to 0.25
- slab_kind: int32 [3], replicated, may hold values from 0 to 2, as said below
- kz_table: int32 [4, 4], replicated, may hold values from 0 to 3, as said below
- mode_weight: float32 [2, 4], replicated, may hold values from 0.25 to 2
- form_factor: float32 [2, 128, 128], replicated, as said below
- occupation: float32 [2], replicated, may hold values from 0.1 to 2
- energy_offset: int32 [2], replicated, may hold values from 1 to 4, as said below
Outputs:
- sigma_less_new: bfloat16 [4, 128, 3, 2, 128, 128], P('kz', 'en')
- sigma_great_new: bfloat16 [4, 128, 3, 2, 128, 128], P('kz', 'en')
The draws below stay inside these ranges and needn't reach their ends.
Inputs may be any that keep to these rules, and one draw needn't show every extreme that they name: `sigma_less`: each block is i times a Hermitian matrix. `sigma_great`: each block is -i times a Hermitian matrix. `onsite_table`: each block is symmetric. `cos_coupling`: each block is symmetric. `form_factor`: each block is symmetric and positive. `kz_table`: each row names every momentum once. `slab_kind`: every kind is used by some slab. `energy_offset`: the modes have different offsets, and some mode has exactly 4.
All inputs are finite; a program needn't handle non-finite values.
Results may differ from the reference program's by a relative error of at most 0.0029.
Values may be sent and summed in bfloat16 or wider, within the bound.
No kernel may reach another device: no remote copies, remote signals or barrier semaphores. Data moves between devices by JAX's collectives and lax.ppermute only.
A program may use at most 128 MiB of HBM per device.

```python
import math
import jax
import jax.numpy as jnp
from jax import lax

M = 128
S = 3
MODES = 2
KINDS = 3
OFFMAX = 4
K = 4
ENERGIES = 128


OFFDIAG = 0.02


def hermitian_parts(key):
    key_diag, key_sym, key_anti = jax.random.split(key, 3)
    shape_full = (K, ENERGIES, S, M, M)
    identity = jnp.eye(M, dtype=jnp.float32)
    diag_values = jax.random.uniform(key_diag, (K, ENERGIES, S, M, 1), jnp.float32, 0.2, 1.0)
    sym_noise = jax.random.normal(key_sym, shape_full, jnp.float32)
    anti_noise = jax.random.normal(key_anti, shape_full, jnp.float32)
    off_mask = 1.0 - identity
    real_part = identity * diag_values + off_mask * OFFDIAG * (sym_noise + jnp.swapaxes(sym_noise, -1, -2)) * 0.70710678
    imag_part = off_mask * OFFDIAG * (anti_noise - jnp.swapaxes(anti_noise, -1, -2)) * 0.70710678
    return (real_part, imag_part)


def draw_sigma_less(key, part):
    real_part, imag_part = hermitian_parts(jax.random.fold_in(key, 11))
    return jnp.stack([-imag_part, real_part], axis=-3).astype(jnp.bfloat16)


def draw_sigma_great(key, part):
    real_part, imag_part = hermitian_parts(jax.random.fold_in(key, 23))
    return jnp.stack([imag_part, -real_part], axis=-3).astype(jnp.bfloat16)


def symmetric_noise(key, leading, scale_value):
    noise = jax.random.normal(key, (leading, M, M), jnp.float32)
    return scale_value * (noise + jnp.swapaxes(noise, -1, -2)) * 0.70710678 / jnp.sqrt(jnp.float32(M))


def draw_onsite_table(key, part):
    return symmetric_noise(jax.random.fold_in(key, 31), KINDS, 1.0)


def draw_cos_coupling(key, part):
    return symmetric_noise(jax.random.fold_in(key, 37), S, 0.5)


def draw_form_factor(key, part):
    base_values = jax.random.uniform(jax.random.fold_in(key, 41), (MODES, M, M), jnp.float32, -1.0, 1.0)
    return jnp.exp(0.5 * (base_values + jnp.swapaxes(base_values, -1, -2)))


def draw_kz_table(key, part):
    row_keys = jax.random.split(jax.random.fold_in(key, 43), K)
    return jax.vmap(lambda row_key: jax.random.permutation(row_key, K))(row_keys).astype(jnp.int32)


def draw_slab_kind(key, part):
    order_drawn = jax.random.permutation(jax.random.fold_in(key, 53), S).astype(jnp.int32)
    return (order_drawn % KINDS).astype(jnp.int32)


def draw_energy_offset(key, part):
    key_values, key_pick = jax.random.split(jax.random.fold_in(key, 47))
    values_drawn = jax.random.randint(key_values, (MODES,), 1, OFFMAX, jnp.int32)
    picked = jax.random.randint(key_pick, (), 0, MODES, jnp.int32)
    return jnp.where(jnp.arange(MODES, dtype=jnp.int32) == picked, OFFMAX, values_drawn).astype(jnp.int32)


def bell_draw(rng, extent, scale, bound, held_as=jnp.bfloat16):
    return jnp.clip(scale * jax.random.normal(rng, extent, jnp.float32), -bound, bound).astype(held_as)


def setup_inputs(seed: int = 0) -> dict:
    key_list = jax.random.split(jax.random.key(seed), 12)
    return {
        "sigma_less": draw_sigma_less(jax.random.fold_in(key_list[11], 71), 0),
        "sigma_great": draw_sigma_great(jax.random.fold_in(key_list[11], 71), 0),
        "onsite_table": draw_onsite_table(jax.random.fold_in(key_list[11], 71), 0),
        "cos_coupling": draw_cos_coupling(jax.random.fold_in(key_list[11], 71), 0),
        "slab_coupling": bell_draw(key_list[4], (S - 1, M, M), (4 * M) ** -0.5, 0.25, jnp.float32),
        "slab_kind": draw_slab_kind(jax.random.fold_in(key_list[11], 71), 0),
        "kz_table": draw_kz_table(jax.random.fold_in(key_list[11], 71), 0),
        "mode_weight": jnp.clip(jnp.exp(jax.random.uniform(key_list[7], (MODES, K), jnp.float32, math.log(0.25), math.log(2.0))), 0.25, 2.0),
        "form_factor": draw_form_factor(jax.random.fold_in(key_list[11], 71), 0),
        "occupation": jnp.clip(jnp.exp(jax.random.uniform(key_list[9], (MODES,), jnp.float32, math.log(0.1), math.log(2.0))), 0.1, 2.0),
        "energy_offset": draw_energy_offset(jax.random.fold_in(key_list[11], 71), 0),
    }


DAMPING = 0.3

def matmul_high(left_matrix, right_matrix):
    return jnp.matmul(left_matrix, right_matrix, precision=lax.Precision.HIGHEST)

def complex_product(left_pair, right_pair):
    real_part = matmul_high(left_pair[0], right_pair[0]) - matmul_high(left_pair[1], right_pair[1])
    imag_part = matmul_high(left_pair[0], right_pair[1]) + matmul_high(left_pair[1], right_pair[0])
    return (real_part, imag_part)

def real_left(matrix, pair_value):
    return (matmul_high(matrix, pair_value[0]), matmul_high(matrix, pair_value[1]))

def real_right(pair_value, matrix):
    return (matmul_high(pair_value[0], matrix), matmul_high(pair_value[1], matrix))

def adjoint(pair_value):
    return (jnp.swapaxes(pair_value[0], -1, -2), -jnp.swapaxes(pair_value[1], -1, -2))

def add_pair(left_pair, right_pair):
    return (left_pair[0] + right_pair[0], left_pair[1] + right_pair[1])

def sub_pair(left_pair, right_pair):
    return (left_pair[0] - right_pair[0], left_pair[1] - right_pair[1])

def invert_pair(pair_value):
    orbitals = pair_value[0].shape[-1]
    upper_half = jnp.concatenate([pair_value[0], -pair_value[1]], axis=-1)
    lower_half = jnp.concatenate([pair_value[1], pair_value[0]], axis=-1)
    embedded = jnp.concatenate([upper_half, lower_half], axis=-2)
    transposed = jnp.swapaxes(embedded, -1, -2)
    normal = matmul_high(transposed, embedded)
    factor = jnp.linalg.cholesky(normal)
    solved = jax.scipy.linalg.cho_solve((factor, True), transposed)
    return (solved[..., :orbitals, :orbitals], solved[..., orbitals:, :orbitals])

def greater_of(less_pair, ret_pair):
    return sub_pair(add_pair(less_pair, ret_pair), adjoint(ret_pair))

def pack_pair(pair_value):
    return jnp.stack([pair_value[0], pair_value[1]], axis=-3)

def green_blocks(sigma_less, sigma_great, hamilton, slab_coupling, energies):
    orbitals = sigma_less.shape[-1]
    slab_count = sigma_less.shape[2]
    identity = jnp.eye(orbitals, dtype=jnp.float32)
    energy_grid = energies[None, :, None, None]
    left_ret = []
    left_less = []
    for slab_index in range(slab_count):
        lesser = sigma_less[:, :, slab_index].astype(jnp.float32)
        greater = sigma_great[:, :, slab_index].astype(jnp.float32)
        retarded_re = 0.5 * (greater[:, :, 0] - lesser[:, :, 0])
        retarded_im = 0.5 * (greater[:, :, 1] - lesser[:, :, 1]) - DAMPING * identity
        system_re = energy_grid * identity - hamilton[:, :, slab_index] - retarded_re
        system_im = -retarded_im
        source = (lesser[:, :, 0], lesser[:, :, 1])
        if slab_index > 0:
            coupling = slab_coupling[slab_index - 1]
            folded = real_right(real_left(coupling, left_ret[-1]), coupling.T)
            system_re = system_re - folded[0]
            system_im = system_im - folded[1]
            source = add_pair(source, real_right(real_left(coupling, left_less[-1]), coupling.T))
        inverse = invert_pair((system_re, system_im))
        left_ret.append(inverse)
        left_less.append(complex_product(complex_product(inverse, source), adjoint(inverse)))
    full_ret = left_ret[-1]
    full_less = left_less[-1]
    lesser_list = [full_less]
    greater_list = [greater_of(full_less, full_ret)]
    for slab_index in range(slab_count - 2, -1, -1):
        coupling = slab_coupling[slab_index]
        green_couple = real_right(left_ret[slab_index], coupling)
        bridge = real_right(complex_product(green_couple, full_ret), coupling.T)
        cross_term = complex_product(bridge, left_less[slab_index])
        spread = complex_product(real_right(complex_product(green_couple, full_less), coupling.T), adjoint(left_ret[slab_index]))
        full_less = add_pair(add_pair(left_less[slab_index], spread), sub_pair(cross_term, adjoint(cross_term)))
        full_ret = add_pair(left_ret[slab_index], complex_product(bridge, left_ret[slab_index]))
        lesser_list.insert(0, full_less)
        greater_list.insert(0, greater_of(full_less, full_ret))
    lesser_all = jnp.stack([pack_pair(item) for item in lesser_list], axis=2)
    greater_all = jnp.stack([pack_pair(item) for item in greater_list], axis=2)
    return jnp.stack([lesser_all, greater_all], axis=2).astype(jnp.bfloat16)

def hamiltonian(onsite_table, cos_coupling, slab_kind, momenta_index, momenta_total):
    kind_count = onsite_table.shape[0]
    choose = (slab_kind[:, None] == jnp.arange(kind_count, dtype=jnp.int32)[None, :]).astype(jnp.float32)
    onsite = jnp.einsum('sk,kij->sij', choose, onsite_table, precision=lax.Precision.HIGHEST)
    phase_factor = jnp.cos(2.0 * jnp.pi * momenta_index.astype(jnp.float32) / momenta_total)
    hamilton = onsite[None] + phase_factor[:, None, None, None] * cos_coupling[None]
    return hamilton[:, None]

def momentum_weights(table_rows, mode_weight, momenta_total):
    onehot = (table_rows[:, :, None] == jnp.arange(momenta_total, dtype=jnp.int32)[None, None, :]).astype(jnp.float32)
    return jnp.einsum('lq,aqk->lak', mode_weight, onehot, precision=lax.Precision.HIGHEST) / momenta_total

def scatter_terms(extended, weights, form_factor, occupation, energy_offset, energy_count, margin):
    total_less = None
    total_great = None
    for mode_index in range(form_factor.shape[0]):
        shift_steps = energy_offset[mode_index]
        upper_side = lax.dynamic_slice_in_dim(extended, margin + shift_steps, energy_count, 1)
        lower_side = lax.dynamic_slice_in_dim(extended, margin - shift_steps, energy_count, 1)
        occupied = occupation[mode_index]
        less_term = (occupied + 1.0) * upper_side[:, :, 0].astype(jnp.float32) + occupied * lower_side[:, :, 0].astype(jnp.float32)
        great_term = (occupied + 1.0) * lower_side[:, :, 1].astype(jnp.float32) + occupied * upper_side[:, :, 1].astype(jnp.float32)
        less_sum = form_factor[mode_index] * jnp.einsum('ak,kesrij->aesrij', weights[mode_index], less_term, precision=lax.Precision.HIGHEST)
        great_sum = form_factor[mode_index] * jnp.einsum('ak,kesrij->aesrij', weights[mode_index], great_term, precision=lax.Precision.HIGHEST)
        total_less = less_sum if total_less is None else total_less + less_sum
        total_great = great_sum if total_great is None else total_great + great_sum
    return (total_less.astype(jnp.bfloat16), total_great.astype(jnp.bfloat16))

def reference(sigma_less, sigma_great, onsite_table, cos_coupling, slab_coupling, slab_kind, kz_table, mode_weight, form_factor, occupation, energy_offset):
    momenta = jnp.arange(K, dtype=jnp.int32)
    hamilton = hamiltonian(onsite_table, cos_coupling, slab_kind, momenta, K)
    energies = -1.5 + 3.0 * (jnp.arange(ENERGIES, dtype=jnp.int32).astype(jnp.float32) + 0.5) / ENERGIES

    def one_momentum(inputs):
        less_one, great_one, hamilton_one = inputs
        return green_blocks(less_one[None], great_one[None], hamilton_one[None], slab_coupling, energies)[0]
    blocks = lax.map(one_momentum, (sigma_less, sigma_great, hamilton))
    extended = jnp.pad(blocks, ((0, 0), (OFFMAX, OFFMAX), (0, 0), (0, 0), (0, 0), (0, 0), (0, 0)))
    weights = momentum_weights(kz_table, mode_weight, K)
    return scatter_terms(extended, weights, form_factor, occupation, energy_offset, ENERGIES, OFFMAX)
```

```python
import jax
import jax.numpy as jnp
from jax import lax
from jax.sharding import PartitionSpec as P
from jax.experimental import pallas as pl

OFFMAX = 4


DAMPING = 0.3


def padded(block, sides, width):
    for axis, dim in sides:
        count = lax.axis_size(axis)
        forward = [(i, i + 1) for i in range(count - 1)]
        backward = [(target, source) for source, target in forward]
        low = lax.ppermute(
            lax.slice_in_dim(block, block.shape[dim] - width, None, axis=dim), axis, forward
        )
        high = lax.ppermute(lax.slice_in_dim(block, 0, width, axis=dim), axis, backward)
        block = jnp.concatenate([low, block, high], axis=dim)
    return block


def matmul_high(left_matrix, right_matrix):
    return jnp.matmul(left_matrix, right_matrix, precision=lax.Precision.HIGHEST)


def complex_product(left_pair, right_pair):
    real_part = matmul_high(left_pair[0], right_pair[0]) - matmul_high(left_pair[1], right_pair[1])
    imag_part = matmul_high(left_pair[0], right_pair[1]) + matmul_high(left_pair[1], right_pair[0])
    return (real_part, imag_part)


def real_left(matrix, pair_value):
    return (matmul_high(matrix, pair_value[0]), matmul_high(matrix, pair_value[1]))


def real_right(pair_value, matrix):
    return (matmul_high(pair_value[0], matrix), matmul_high(pair_value[1], matrix))


def adjoint(pair_value):
    return (jnp.swapaxes(pair_value[0], -1, -2), -jnp.swapaxes(pair_value[1], -1, -2))


def add_pair(left_pair, right_pair):
    return (left_pair[0] + right_pair[0], left_pair[1] + right_pair[1])


def sub_pair(left_pair, right_pair):
    return (left_pair[0] - right_pair[0], left_pair[1] - right_pair[1])


def sweep_kernel(normal_re_ref, normal_im_ref, out_re_ref, out_im_ref):
    batch, orbitals, _ = normal_re_ref.shape
    out_re_ref[...] = normal_re_ref[...]
    out_im_ref[...] = normal_im_ref[...]
    lane = lax.broadcasted_iota(jnp.int32, (1, orbitals), 1)
    row_index = lax.broadcasted_iota(jnp.int32, (orbitals, 1), 0)

    def step(pivot, carry):
        lane_hit = lane == pivot
        row_hit = row_index == pivot
        for item in range(batch):
            whole_re = out_re_ref[item]
            whole_im = out_im_ref[item]
            row_re = out_re_ref[item, pl.ds(pivot, 1), :]
            row_im = out_im_ref[item, pl.ds(pivot, 1), :]
            col_re = jnp.sum(jnp.where(lane_hit, whole_re, 0.0), axis=1, keepdims=True)
            col_im = jnp.sum(jnp.where(lane_hit, whole_im, 0.0), axis=1, keepdims=True)
            piv_re = jnp.sum(jnp.where(lane_hit, row_re, 0.0), axis=1, keepdims=True)
            piv_im = jnp.sum(jnp.where(lane_hit, row_im, 0.0), axis=1, keepdims=True)
            norm = piv_re * piv_re + piv_im * piv_im
            inv_re = piv_re / norm
            inv_im = -piv_im / norm
            scaled_re = jnp.where(lane_hit, inv_re, row_re * inv_re - row_im * inv_im)
            scaled_im = jnp.where(lane_hit, inv_im, row_re * inv_im + row_im * inv_re)
            col_re = jnp.where(row_hit, 0.0, col_re)
            col_im = jnp.where(row_hit, 0.0, col_im)
            base_re = jnp.where(lane_hit, 0.0, whole_re)
            base_im = jnp.where(lane_hit, 0.0, whole_im)
            out_re_ref[item] = base_re - (col_re * scaled_re - col_im * scaled_im)
            out_im_ref[item] = base_im - (col_re * scaled_im + col_im * scaled_re)
            out_re_ref[item, pl.ds(pivot, 1), :] = scaled_re
            out_im_ref[item, pl.ds(pivot, 1), :] = scaled_im
        return carry

    lax.fori_loop(0, orbitals, step, 0)


def hermitian_inverse(normal_pair, interpret=False):
    shape = normal_pair[0].shape
    orbitals = shape[-1]
    flat = [item.reshape(-1, orbitals, orbitals) for item in normal_pair]
    out_shape = jax.ShapeDtypeStruct(flat[0].shape, jnp.float32)
    inverse = pl.pallas_call(
        sweep_kernel,
        out_shape=(out_shape, out_shape),
        interpret=interpret,
    )(*flat)
    return (inverse[0].reshape(shape), inverse[1].reshape(shape))


def invert_pair(pair_value, interpret=False):
    adjoint_value = adjoint(pair_value)
    normal = complex_product(adjoint_value, pair_value)
    normal_inverse = hermitian_inverse(normal, interpret)
    return complex_product(normal_inverse, adjoint_value)


def greater_of(less_pair, ret_pair):
    return sub_pair(add_pair(less_pair, ret_pair), adjoint(ret_pair))


def pack_pair(pair_value):
    return jnp.stack([pair_value[0], pair_value[1]], axis=-3)


def green_blocks(sigma_less, sigma_great, hamilton, slab_coupling, energies):
    orbitals = sigma_less.shape[-1]
    slab_count = sigma_less.shape[2]
    identity = jnp.eye(orbitals, dtype=jnp.float32)
    energy_grid = energies[None, :, None, None]
    left_ret = []
    left_less = []
    for slab_index in range(slab_count):
        lesser = sigma_less[:, :, slab_index].astype(jnp.float32)
        greater = sigma_great[:, :, slab_index].astype(jnp.float32)
        retarded_re = 0.5 * (greater[:, :, 0] - lesser[:, :, 0])
        retarded_im = 0.5 * (greater[:, :, 1] - lesser[:, :, 1]) - DAMPING * identity
        system_re = energy_grid * identity - hamilton[:, :, slab_index] - retarded_re
        system_im = -retarded_im
        source = (lesser[:, :, 0], lesser[:, :, 1])
        if slab_index > 0:
            coupling = slab_coupling[slab_index - 1]
            folded = real_right(real_left(coupling, left_ret[-1]), coupling.T)
            system_re = system_re - folded[0]
            system_im = system_im - folded[1]
            source = add_pair(source, real_right(real_left(coupling, left_less[-1]), coupling.T))
        inverse = invert_pair((system_re, system_im))
        left_ret.append(inverse)
        left_less.append(complex_product(complex_product(inverse, source), adjoint(inverse)))
    full_ret = left_ret[-1]
    full_less = left_less[-1]
    lesser_list = [full_less]
    greater_list = [greater_of(full_less, full_ret)]
    for slab_index in range(slab_count - 2, -1, -1):
        coupling = slab_coupling[slab_index]
        green_couple = real_right(left_ret[slab_index], coupling)
        bridge = real_right(complex_product(green_couple, full_ret), coupling.T)
        cross_term = complex_product(bridge, left_less[slab_index])
        spread = complex_product(
            real_right(complex_product(green_couple, full_less), coupling.T),
            adjoint(left_ret[slab_index]),
        )
        full_less = add_pair(
            add_pair(left_less[slab_index], spread), sub_pair(cross_term, adjoint(cross_term))
        )
        full_ret = add_pair(left_ret[slab_index], complex_product(bridge, left_ret[slab_index]))
        lesser_list.insert(0, full_less)
        greater_list.insert(0, greater_of(full_less, full_ret))
    lesser_all = jnp.stack([pack_pair(item) for item in lesser_list], axis=2)
    greater_all = jnp.stack([pack_pair(item) for item in greater_list], axis=2)
    return jnp.stack([lesser_all, greater_all], axis=2).astype(jnp.bfloat16)


def hamiltonian(onsite_table, cos_coupling, slab_kind, momenta_index, momenta_total):
    kind_count = onsite_table.shape[0]
    choose = (slab_kind[:, None] == jnp.arange(kind_count, dtype=jnp.int32)[None, :]).astype(
        jnp.float32
    )
    onsite = jnp.einsum("sk,kij->sij", choose, onsite_table, precision=lax.Precision.HIGHEST)
    phase_factor = jnp.cos(2.0 * jnp.pi * momenta_index.astype(jnp.float32) / momenta_total)
    hamilton = onsite[None] + phase_factor[:, None, None, None] * cos_coupling[None]
    return hamilton[:, None]


def momentum_weights(table_rows, mode_weight, momenta_total):
    onehot = (
        table_rows[:, :, None] == jnp.arange(momenta_total, dtype=jnp.int32)[None, None, :]
    ).astype(jnp.float32)
    return (
        jnp.einsum("lq,aqk->lak", mode_weight, onehot, precision=lax.Precision.HIGHEST)
        / momenta_total
    )


def mixed_sums(extended, weights, form_factor, occupation, energy_offset, energy_count, margin):
    total_less = None
    total_great = None
    for mode_index in range(form_factor.shape[0]):
        shift_steps = energy_offset[mode_index]
        upper_side = lax.dynamic_slice_in_dim(extended, margin + shift_steps, energy_count, 1)
        lower_side = lax.dynamic_slice_in_dim(extended, margin - shift_steps, energy_count, 1)
        occupied = occupation[mode_index]
        less_term = (occupied + 1.0) * upper_side[:, :, 0].astype(
            jnp.float32
        ) + occupied * lower_side[:, :, 0].astype(jnp.float32)
        great_term = (occupied + 1.0) * lower_side[:, :, 1].astype(
            jnp.float32
        ) + occupied * upper_side[:, :, 1].astype(jnp.float32)
        less_sum = form_factor[mode_index] * jnp.einsum(
            "ak,kesrij->aesrij", weights[mode_index], less_term, precision=lax.Precision.HIGHEST
        )
        great_sum = form_factor[mode_index] * jnp.einsum(
            "ak,kesrij->aesrij", weights[mode_index], great_term, precision=lax.Precision.HIGHEST
        )
        total_less = less_sum if total_less is None else total_less + less_sum
        total_great = great_sum if total_great is None else total_great + great_sum
    return (total_less, total_great)


def on_device(
    sigma_less,
    sigma_great,
    onsite_table,
    cos_coupling,
    slab_coupling,
    slab_kind,
    kz_table,
    mode_weight,
    form_factor,
    occupation,
    energy_offset,
):
    momenta_local = sigma_less.shape[0]
    energy_local = sigma_less.shape[1]
    momenta_total = momenta_local * lax.axis_size("kz")
    energy_total = energy_local * lax.axis_size("en")
    momenta_start = lax.axis_index("kz") * momenta_local
    momenta_index = momenta_start + jnp.arange(momenta_local, dtype=jnp.int32)
    energy_index = lax.axis_index("en") * energy_local + jnp.arange(energy_local, dtype=jnp.int32)
    energies = -1.5 + 3.0 * (energy_index.astype(jnp.float32) + 0.5) / energy_total
    hamilton = hamiltonian(onsite_table, cos_coupling, slab_kind, momenta_index, momenta_total)
    blocks = green_blocks(sigma_less, sigma_great, hamilton, slab_coupling, energies)
    table_rows = lax.dynamic_slice_in_dim(kz_table, momenta_start, momenta_local, 0)
    weights = momentum_weights(table_rows, mode_weight, momenta_total)
    everyone = lax.all_gather(blocks, "kz", axis=0, tiled=True)
    extended = padded(everyone, (("en", 1),), OFFMAX)
    less_total, great_total = mixed_sums(
        extended, weights, form_factor, occupation, energy_offset, energy_local, OFFMAX
    )
    return (less_total.astype(jnp.bfloat16), great_total.astype(jnp.bfloat16))


def solution(mesh):
    in_specs = (
        P("kz", "en", None, None, None, None),
        P("kz", "en", None, None, None, None),
        P(),
        P(),
        P(),
        P(),
        P(),
        P(),
        P(),
        P(),
        P(),
    )
    out_specs = (P("kz", "en", None, None, None, None), P("kz", "en", None, None, None, None))
    return jax.shard_map(
        on_device, mesh=mesh, in_specs=in_specs, out_specs=out_specs, check_vma=False
    )
```

```python
import jax
import jax.numpy as jnp
from jax import lax
from jax.sharding import PartitionSpec as P
from jax.experimental import pallas as pl

OFFMAX = 4


DAMPING = 0.3


def padded(block, sides, width):
    for axis, dim in sides:
        count = lax.axis_size(axis)
        forward = [(i, i + 1) for i in range(count - 1)]
        backward = [(target, source) for source, target in forward]
        low = lax.ppermute(
            lax.slice_in_dim(block, block.shape[dim] - width, None, axis=dim), axis, forward
        )
        high = lax.ppermute(lax.slice_in_dim(block, 0, width, axis=dim), axis, backward)
        block = jnp.concatenate([low, block, high], axis=dim)
    return block


def matmul_high(left_matrix, right_matrix):
    return jnp.matmul(left_matrix, right_matrix, precision=lax.Precision.HIGHEST)


def complex_product(left_pair, right_pair):
    real_part = matmul_high(left_pair[0], right_pair[0]) - matmul_high(left_pair[1], right_pair[1])
    imag_part = matmul_high(left_pair[0], right_pair[1]) + matmul_high(left_pair[1], right_pair[0])
    return (real_part, imag_part)


def real_left(matrix, pair_value):
    return (matmul_high(matrix, pair_value[0]), matmul_high(matrix, pair_value[1]))


def real_right(pair_value, matrix):
    return (matmul_high(pair_value[0], matrix), matmul_high(pair_value[1], matrix))


def adjoint(pair_value):
    return (jnp.swapaxes(pair_value[0], -1, -2), -jnp.swapaxes(pair_value[1], -1, -2))


def add_pair(left_pair, right_pair):
    return (left_pair[0] + right_pair[0], left_pair[1] + right_pair[1])


def sub_pair(left_pair, right_pair):
    return (left_pair[0] - right_pair[0], left_pair[1] - right_pair[1])


def sweep_kernel(normal_re_ref, normal_im_ref, out_re_ref, out_im_ref):
    batch, orbitals, _ = normal_re_ref.shape
    out_re_ref[...] = normal_re_ref[...]
    out_im_ref[...] = normal_im_ref[...]
    lane = lax.broadcasted_iota(jnp.int32, (1, orbitals), 1)
    row_index = lax.broadcasted_iota(jnp.int32, (orbitals, 1), 0)

    def step(pivot, carry):
        lane_hit = lane == pivot
        row_hit = row_index == pivot
        for item in range(batch):
            whole_re = out_re_ref[item]
            whole_im = out_im_ref[item]
            row_re = out_re_ref[item, pl.ds(pivot, 1), :]
            row_im = out_im_ref[item, pl.ds(pivot, 1), :]
            col_re = jnp.sum(jnp.where(lane_hit, whole_re, 0.0), axis=1, keepdims=True)
            col_im = jnp.sum(jnp.where(lane_hit, whole_im, 0.0), axis=1, keepdims=True)
            piv_re = jnp.sum(jnp.where(lane_hit, row_re, 0.0), axis=1, keepdims=True)
            piv_im = jnp.sum(jnp.where(lane_hit, row_im, 0.0), axis=1, keepdims=True)
            norm = piv_re * piv_re + piv_im * piv_im
            inv_re = piv_re / norm
            inv_im = -piv_im / norm
            scaled_re = jnp.where(lane_hit, inv_re, row_re * inv_re - row_im * inv_im)
            scaled_im = jnp.where(lane_hit, inv_im, row_re * inv_im + row_im * inv_re)
            col_re = jnp.where(row_hit, 0.0, col_re)
            col_im = jnp.where(row_hit, 0.0, col_im)
            base_re = jnp.where(lane_hit, 0.0, whole_re)
            base_im = jnp.where(lane_hit, 0.0, whole_im)
            out_re_ref[item] = base_re - (col_re * scaled_re - col_im * scaled_im)
            out_im_ref[item] = base_im - (col_re * scaled_im + col_im * scaled_re)
            out_re_ref[item, pl.ds(pivot, 1), :] = scaled_re
            out_im_ref[item, pl.ds(pivot, 1), :] = scaled_im
        return carry

    lax.fori_loop(0, orbitals, step, 0)


def hermitian_inverse(normal_pair, interpret=False):
    shape = normal_pair[0].shape
    orbitals = shape[-1]
    flat = [item.reshape(-1, orbitals, orbitals) for item in normal_pair]
    out_shape = jax.ShapeDtypeStruct(flat[0].shape, jnp.float32)
    inverse = pl.pallas_call(
        sweep_kernel,
        out_shape=(out_shape, out_shape),
        interpret=interpret,
    )(*flat)
    return (inverse[0].reshape(shape), inverse[1].reshape(shape))


def invert_pair(pair_value, interpret=False):
    adjoint_value = adjoint(pair_value)
    normal = complex_product(adjoint_value, pair_value)
    normal_inverse = hermitian_inverse(normal, interpret)
    return complex_product(normal_inverse, adjoint_value)


def greater_of(less_pair, ret_pair):
    return sub_pair(add_pair(less_pair, ret_pair), adjoint(ret_pair))


def pack_pair(pair_value):
    return jnp.stack([pair_value[0], pair_value[1]], axis=-3)


def green_blocks(sigma_less, sigma_great, hamilton, slab_coupling, energies):
    orbitals = sigma_less.shape[-1]
    slab_count = sigma_less.shape[2]
    identity = jnp.eye(orbitals, dtype=jnp.float32)
    energy_grid = energies[None, :, None, None]
    left_ret = []
    left_less = []
    for slab_index in range(slab_count):
        lesser = sigma_less[:, :, slab_index].astype(jnp.float32)
        greater = sigma_great[:, :, slab_index].astype(jnp.float32)
        retarded_re = 0.5 * (greater[:, :, 0] - lesser[:, :, 0])
        retarded_im = 0.5 * (greater[:, :, 1] - lesser[:, :, 1]) - DAMPING * identity
        system_re = energy_grid * identity - hamilton[:, :, slab_index] - retarded_re
        system_im = -retarded_im
        source = (lesser[:, :, 0], lesser[:, :, 1])
        if slab_index > 0:
            coupling = slab_coupling[slab_index - 1]
            folded = real_right(real_left(coupling, left_ret[-1]), coupling.T)
            system_re = system_re - folded[0]
            system_im = system_im - folded[1]
            source = add_pair(source, real_right(real_left(coupling, left_less[-1]), coupling.T))
        inverse = invert_pair((system_re, system_im))
        left_ret.append(inverse)
        left_less.append(complex_product(complex_product(inverse, source), adjoint(inverse)))
    full_ret = left_ret[-1]
    full_less = left_less[-1]
    lesser_list = [full_less]
    greater_list = [greater_of(full_less, full_ret)]
    for slab_index in range(slab_count - 2, -1, -1):
        coupling = slab_coupling[slab_index]
        green_couple = real_right(left_ret[slab_index], coupling)
        bridge = real_right(complex_product(green_couple, full_ret), coupling.T)
        cross_term = complex_product(bridge, left_less[slab_index])
        spread = complex_product(
            real_right(complex_product(green_couple, full_less), coupling.T),
            adjoint(left_ret[slab_index]),
        )
        full_less = add_pair(
            add_pair(left_less[slab_index], spread), sub_pair(cross_term, adjoint(cross_term))
        )
        full_ret = add_pair(left_ret[slab_index], complex_product(bridge, left_ret[slab_index]))
        lesser_list.insert(0, full_less)
        greater_list.insert(0, greater_of(full_less, full_ret))
    lesser_all = jnp.stack([pack_pair(item) for item in lesser_list], axis=2)
    greater_all = jnp.stack([pack_pair(item) for item in greater_list], axis=2)
    return jnp.stack([lesser_all, greater_all], axis=2).astype(jnp.bfloat16)


def hamiltonian(onsite_table, cos_coupling, slab_kind, momenta_index, momenta_total):
    kind_count = onsite_table.shape[0]
    choose = (slab_kind[:, None] == jnp.arange(kind_count, dtype=jnp.int32)[None, :]).astype(
        jnp.float32
    )
    onsite = jnp.einsum("sk,kij->sij", choose, onsite_table, precision=lax.Precision.HIGHEST)
    phase_factor = jnp.cos(2.0 * jnp.pi * momenta_index.astype(jnp.float32) / momenta_total)
    hamilton = onsite[None] + phase_factor[:, None, None, None] * cos_coupling[None]
    return hamilton[:, None]


def momentum_weights(table_rows, mode_weight, momenta_total):
    onehot = (
        table_rows[:, :, None] == jnp.arange(momenta_total, dtype=jnp.int32)[None, None, :]
    ).astype(jnp.float32)
    return (
        jnp.einsum("lq,aqk->lak", mode_weight, onehot, precision=lax.Precision.HIGHEST)
        / momenta_total
    )


def mixed_sums(extended, weights, form_factor, occupation, energy_offset, energy_count, margin):
    total_less = None
    total_great = None
    for mode_index in range(form_factor.shape[0]):
        shift_steps = energy_offset[mode_index]
        upper_side = lax.dynamic_slice_in_dim(extended, margin + shift_steps, energy_count, 1)
        lower_side = lax.dynamic_slice_in_dim(extended, margin - shift_steps, energy_count, 1)
        occupied = occupation[mode_index]
        less_term = (occupied + 1.0) * upper_side[:, :, 0].astype(
            jnp.float32
        ) + occupied * lower_side[:, :, 0].astype(jnp.float32)
        great_term = (occupied + 1.0) * lower_side[:, :, 1].astype(
            jnp.float32
        ) + occupied * upper_side[:, :, 1].astype(jnp.float32)
        mode_weights = weights[mode_index][:, :, None, None, None, None, None]
        less_sum = form_factor[mode_index] * jnp.sum(mode_weights * less_term[None], axis=1)
        great_sum = form_factor[mode_index] * jnp.sum(mode_weights * great_term[None], axis=1)
        total_less = less_sum if total_less is None else total_less + less_sum
        total_great = great_sum if total_great is None else total_great + great_sum
    return (total_less, total_great)


def exchange_blocks(blocks, width):
    count = lax.axis_size("kz")
    momentum = lax.axis_index("kz")
    far_pairs = [(i, (i + 2) % count) for i in range(count)]
    near_pairs = [(i, i ^ 1) for i in range(count)]
    far = lax.ppermute(blocks, "kz", far_pairs)
    local_pair = jnp.concatenate([blocks, far], axis=0)
    extended = padded(local_pair, (("en", 1),), width)
    other = lax.ppermute(extended, "kz", near_pairs)
    everyone = jnp.concatenate([extended, other], axis=0)
    partner = momentum ^ 1
    order = jnp.stack([momentum, (momentum + 2) % count, partner, (partner + 2) % count])
    return everyone, order


def on_device(
    sigma_less,
    sigma_great,
    onsite_table,
    cos_coupling,
    slab_coupling,
    slab_kind,
    kz_table,
    mode_weight,
    form_factor,
    occupation,
    energy_offset,
):
    momenta_local = sigma_less.shape[0]
    energy_local = sigma_less.shape[1]
    momenta_total = momenta_local * lax.axis_size("kz")
    energy_total = energy_local * lax.axis_size("en")
    momenta_start = lax.axis_index("kz") * momenta_local
    momenta_index = momenta_start + jnp.arange(momenta_local, dtype=jnp.int32)
    energy_index = lax.axis_index("en") * energy_local + jnp.arange(energy_local, dtype=jnp.int32)
    energies = -1.5 + 3.0 * (energy_index.astype(jnp.float32) + 0.5) / energy_total
    hamilton = hamiltonian(onsite_table, cos_coupling, slab_kind, momenta_index, momenta_total)
    blocks = green_blocks(sigma_less, sigma_great, hamilton, slab_coupling, energies)
    table_rows = lax.dynamic_slice_in_dim(kz_table, momenta_start, momenta_local, 0)
    weights = momentum_weights(table_rows, mode_weight, momenta_total)
    extended, order = exchange_blocks(blocks, OFFMAX)
    weights = jnp.take(weights, order, axis=2)
    less_total, great_total = mixed_sums(
        extended, weights, form_factor, occupation, energy_offset, energy_local, OFFMAX
    )
    return (less_total.astype(jnp.bfloat16), great_total.astype(jnp.bfloat16))


def solution(mesh):
    in_specs = (
        P("kz", "en", None, None, None, None),
        P("kz", "en", None, None, None, None),
        P(),
        P(),
        P(),
        P(),
        P(),
        P(),
        P(),
        P(),
        P(),
    )
    out_specs = (P("kz", "en", None, None, None, None), P("kz", "en", None, None, None, None))
    return jax.shard_map(
        on_device, mesh=mesh, in_specs=in_specs, out_specs=out_specs, check_vma=False
    )
```

```python
import jax
import jax.numpy as jnp
from jax import lax
from jax.sharding import PartitionSpec as P
from jax.experimental import pallas as pl

OFFMAX = 4


DAMPING = 0.3


def padded(block, sides, width):
    for axis, dim in sides:
        count = lax.axis_size(axis)
        forward = [(i, i + 1) for i in range(count - 1)]
        backward = [(target, source) for source, target in forward]
        low = lax.ppermute(
            lax.slice_in_dim(block, block.shape[dim] - width, None, axis=dim), axis, forward
        )
        high = lax.ppermute(lax.slice_in_dim(block, 0, width, axis=dim), axis, backward)
        block = jnp.concatenate([low, block, high], axis=dim)
    return block


def matmul_high(left_matrix, right_matrix):
    return jnp.matmul(left_matrix, right_matrix, precision=lax.Precision.HIGHEST)


def complex_product(left_pair, right_pair):
    real_part = matmul_high(left_pair[0], right_pair[0]) - matmul_high(left_pair[1], right_pair[1])
    imag_part = matmul_high(left_pair[0], right_pair[1]) + matmul_high(left_pair[1], right_pair[0])
    return (real_part, imag_part)


def real_left(matrix, pair_value):
    return (matmul_high(matrix, pair_value[0]), matmul_high(matrix, pair_value[1]))


def real_right(pair_value, matrix):
    return (matmul_high(pair_value[0], matrix), matmul_high(pair_value[1], matrix))


def adjoint(pair_value):
    return (jnp.swapaxes(pair_value[0], -1, -2), -jnp.swapaxes(pair_value[1], -1, -2))


def add_pair(left_pair, right_pair):
    return (left_pair[0] + right_pair[0], left_pair[1] + right_pair[1])


def sub_pair(left_pair, right_pair):
    return (left_pair[0] - right_pair[0], left_pair[1] - right_pair[1])


def sweep_kernel(normal_re_ref, normal_im_ref, out_re_ref, out_im_ref):
    batch, orbitals, _ = normal_re_ref.shape
    out_re_ref[...] = normal_re_ref[...]
    out_im_ref[...] = normal_im_ref[...]
    lane = lax.broadcasted_iota(jnp.int32, (1, orbitals), 1)
    row_index = lax.broadcasted_iota(jnp.int32, (orbitals, 1), 0)

    def step(pivot, carry):
        lane_hit = lane == pivot
        row_hit = row_index == pivot
        for item in range(batch):
            whole_re = out_re_ref[item]
            whole_im = out_im_ref[item]
            row_re = out_re_ref[item, pl.ds(pivot, 1), :]
            row_im = out_im_ref[item, pl.ds(pivot, 1), :]
            col_re = jnp.sum(jnp.where(lane_hit, whole_re, 0.0), axis=1, keepdims=True)
            col_im = jnp.sum(jnp.where(lane_hit, whole_im, 0.0), axis=1, keepdims=True)
            piv_re = jnp.sum(jnp.where(lane_hit, row_re, 0.0), axis=1, keepdims=True)
            piv_im = jnp.sum(jnp.where(lane_hit, row_im, 0.0), axis=1, keepdims=True)
            norm = piv_re * piv_re + piv_im * piv_im
            inv_re = piv_re / norm
            inv_im = -piv_im / norm
            scaled_re = jnp.where(lane_hit, inv_re, row_re * inv_re - row_im * inv_im)
            scaled_im = jnp.where(lane_hit, inv_im, row_re * inv_im + row_im * inv_re)
            col_re = jnp.where(row_hit, 0.0, col_re)
            col_im = jnp.where(row_hit, 0.0, col_im)
            base_re = jnp.where(lane_hit, 0.0, whole_re)
            base_im = jnp.where(lane_hit, 0.0, whole_im)
            out_re_ref[item] = base_re - (col_re * scaled_re - col_im * scaled_im)
            out_im_ref[item] = base_im - (col_re * scaled_im + col_im * scaled_re)
            out_re_ref[item, pl.ds(pivot, 1), :] = scaled_re
            out_im_ref[item, pl.ds(pivot, 1), :] = scaled_im
        return carry

    lax.fori_loop(0, orbitals, step, 0)


def hermitian_inverse(normal_pair, interpret=False):
    shape = normal_pair[0].shape
    orbitals = shape[-1]
    flat = [item.reshape(-1, orbitals, orbitals) for item in normal_pair]
    out_shape = jax.ShapeDtypeStruct(flat[0].shape, jnp.float32)
    inverse = pl.pallas_call(
        sweep_kernel,
        out_shape=(out_shape, out_shape),
        interpret=interpret,
    )(*flat)
    return (inverse[0].reshape(shape), inverse[1].reshape(shape))


def invert_pair(pair_value, interpret=False):
    adjoint_value = adjoint(pair_value)
    normal = complex_product(adjoint_value, pair_value)
    normal_inverse = hermitian_inverse(normal, interpret)
    return complex_product(normal_inverse, adjoint_value)


def greater_of(less_pair, ret_pair):
    return sub_pair(add_pair(less_pair, ret_pair), adjoint(ret_pair))


def pack_pair(pair_value):
    return jnp.stack([pair_value[0], pair_value[1]], axis=-3)


def green_blocks(sigma_less, sigma_great, hamilton, slab_coupling, energies):
    orbitals = sigma_less.shape[-1]
    slab_count = sigma_less.shape[2]
    identity = jnp.eye(orbitals, dtype=jnp.float32)
    energy_grid = energies[None, :, None, None]
    left_ret = []
    left_less = []
    for slab_index in range(slab_count):
        lesser = sigma_less[:, :, slab_index].astype(jnp.float32)
        greater = sigma_great[:, :, slab_index].astype(jnp.float32)
        retarded_re = 0.5 * (greater[:, :, 0] - lesser[:, :, 0])
        retarded_im = 0.5 * (greater[:, :, 1] - lesser[:, :, 1]) - DAMPING * identity
        system_re = energy_grid * identity - hamilton[:, :, slab_index] - retarded_re
        system_im = -retarded_im
        source = (lesser[:, :, 0], lesser[:, :, 1])
        if slab_index > 0:
            coupling = slab_coupling[slab_index - 1]
            folded = real_right(real_left(coupling, left_ret[-1]), coupling.T)
            system_re = system_re - folded[0]
            system_im = system_im - folded[1]
            source = add_pair(source, real_right(real_left(coupling, left_less[-1]), coupling.T))
        inverse = invert_pair((system_re, system_im))
        left_ret.append(inverse)
        left_less.append(complex_product(complex_product(inverse, source), adjoint(inverse)))
    full_ret = left_ret[-1]
    full_less = left_less[-1]
    lesser_list = [full_less]
    greater_list = [greater_of(full_less, full_ret)]
    for slab_index in range(slab_count - 2, -1, -1):
        coupling = slab_coupling[slab_index]
        green_couple = real_right(left_ret[slab_index], coupling)
        bridge = real_right(complex_product(green_couple, full_ret), coupling.T)
        cross_term = complex_product(bridge, left_less[slab_index])
        spread = complex_product(
            real_right(complex_product(green_couple, full_less), coupling.T),
            adjoint(left_ret[slab_index]),
        )
        full_less = add_pair(
            add_pair(left_less[slab_index], spread), sub_pair(cross_term, adjoint(cross_term))
        )
        full_ret = add_pair(left_ret[slab_index], complex_product(bridge, left_ret[slab_index]))
        lesser_list.insert(0, full_less)
        greater_list.insert(0, greater_of(full_less, full_ret))
    return [
        jnp.stack([pack_pair(less_item), pack_pair(great_item)], axis=2).astype(jnp.bfloat16)
        for less_item, great_item in zip(lesser_list, greater_list)
    ]


def hamiltonian(onsite_table, cos_coupling, slab_kind, momenta_index, momenta_total):
    kind_count = onsite_table.shape[0]
    choose = (slab_kind[:, None] == jnp.arange(kind_count, dtype=jnp.int32)[None, :]).astype(
        jnp.float32
    )
    onsite = jnp.einsum("sk,kij->sij", choose, onsite_table, precision=lax.Precision.HIGHEST)
    phase_factor = jnp.cos(2.0 * jnp.pi * momenta_index.astype(jnp.float32) / momenta_total)
    hamilton = onsite[None] + phase_factor[:, None, None, None] * cos_coupling[None]
    return hamilton[:, None]


def momentum_weights(table_rows, mode_weight, momenta_total):
    onehot = (
        table_rows[:, :, None] == jnp.arange(momenta_total, dtype=jnp.int32)[None, None, :]
    ).astype(jnp.float32)
    return (
        jnp.einsum("lq,aqk->lak", mode_weight, onehot, precision=lax.Precision.HIGHEST)
        / momenta_total
    )


def mixed_sums(extended, weights, form_factor, occupation, energy_offset, energy_count, margin):
    total_less = None
    total_great = None
    for mode_index in range(form_factor.shape[0]):
        shift_steps = energy_offset[mode_index]
        upper_side = lax.dynamic_slice_in_dim(extended, margin + shift_steps, energy_count, 1)
        lower_side = lax.dynamic_slice_in_dim(extended, margin - shift_steps, energy_count, 1)
        occupied = occupation[mode_index]
        less_term = (occupied + 1.0) * upper_side[:, :, 0].astype(
            jnp.float32
        ) + occupied * lower_side[:, :, 0].astype(jnp.float32)
        great_term = (occupied + 1.0) * lower_side[:, :, 1].astype(
            jnp.float32
        ) + occupied * upper_side[:, :, 1].astype(jnp.float32)
        mode_weights = weights[mode_index].reshape(
            weights.shape[1:] + (1,) * (less_term.ndim - 1)
        )
        less_sum = form_factor[mode_index] * jnp.sum(mode_weights * less_term[None], axis=1)
        great_sum = form_factor[mode_index] * jnp.sum(mode_weights * great_term[None], axis=1)
        total_less = less_sum if total_less is None else total_less + less_sum
        total_great = great_sum if total_great is None else total_great + great_sum
    return (total_less, total_great)


def exchange_blocks(blocks, width):
    count = lax.axis_size("kz")
    momentum = lax.axis_index("kz")
    far_pairs = [(i, (i + 2) % count) for i in range(count)]
    near_pairs = [(i, i ^ 1) for i in range(count)]
    far = lax.ppermute(blocks, "kz", far_pairs)
    own_extended = padded(blocks, (("en", 1),), width)
    far_extended = padded(far, (("en", 1),), width)
    extended = jnp.concatenate([own_extended, far_extended], axis=0)
    other = lax.ppermute(extended, "kz", near_pairs)
    everyone = jnp.concatenate([extended, other], axis=0)
    partner = momentum ^ 1
    order = jnp.stack([momentum, (momentum + 2) % count, partner, (partner + 2) % count])
    return everyone, order


def on_device(
    sigma_less,
    sigma_great,
    onsite_table,
    cos_coupling,
    slab_coupling,
    slab_kind,
    kz_table,
    mode_weight,
    form_factor,
    occupation,
    energy_offset,
):
    momenta_local = sigma_less.shape[0]
    energy_local = sigma_less.shape[1]
    momenta_total = momenta_local * lax.axis_size("kz")
    energy_total = energy_local * lax.axis_size("en")
    momenta_start = lax.axis_index("kz") * momenta_local
    momenta_index = momenta_start + jnp.arange(momenta_local, dtype=jnp.int32)
    energy_index = lax.axis_index("en") * energy_local + jnp.arange(energy_local, dtype=jnp.int32)
    energies = -1.5 + 3.0 * (energy_index.astype(jnp.float32) + 0.5) / energy_total
    hamilton = hamiltonian(onsite_table, cos_coupling, slab_kind, momenta_index, momenta_total)
    slab_blocks = green_blocks(sigma_less, sigma_great, hamilton, slab_coupling, energies)
    table_rows = lax.dynamic_slice_in_dim(kz_table, momenta_start, momenta_local, 0)
    weights = momentum_weights(table_rows, mode_weight, momenta_total)
    less_parts = []
    great_parts = []
    for blocks in slab_blocks:
        extended, order = exchange_blocks(blocks, OFFMAX)
        less_part, great_part = mixed_sums(
            extended,
            jnp.take(weights, order, axis=2),
            form_factor,
            occupation,
            energy_offset,
            energy_local,
            OFFMAX,
        )
        less_parts.append(less_part.astype(jnp.bfloat16))
        great_parts.append(great_part.astype(jnp.bfloat16))
    return (jnp.stack(less_parts, axis=2), jnp.stack(great_parts, axis=2))


def solution(mesh):
    in_specs = (
        P("kz", "en", None, None, None, None),
        P("kz", "en", None, None, None, None),
        P(),
        P(),
        P(),
        P(),
        P(),
        P(),
        P(),
        P(),
        P(),
    )
    out_specs = (P("kz", "en", None, None, None, None), P("kz", "en", None, None, None, None))
    return jax.shard_map(
        on_device, mesh=mesh, in_specs=in_specs, out_specs=out_specs, check_vma=False
    )
```

```python
import jax
import jax.numpy as jnp
from jax import lax
from jax.sharding import PartitionSpec as P
from jax.experimental import pallas as pl

OFFMAX = 4


DAMPING = 0.3


def padded(block, sides, width):
    for axis, dim in sides:
        count = lax.axis_size(axis)
        forward = [(i, i + 1) for i in range(count - 1)]
        backward = [(target, source) for source, target in forward]
        low = lax.ppermute(
            lax.slice_in_dim(block, block.shape[dim] - width, None, axis=dim), axis, forward
        )
        high = lax.ppermute(lax.slice_in_dim(block, 0, width, axis=dim), axis, backward)
        block = jnp.concatenate([low, block, high], axis=dim)
    return block


def matmul_high(left_matrix, right_matrix):
    return jnp.matmul(left_matrix, right_matrix, precision=lax.Precision.HIGHEST)


def complex_product(left_pair, right_pair):
    real_part = matmul_high(left_pair[0], right_pair[0]) - matmul_high(left_pair[1], right_pair[1])
    imag_part = matmul_high(left_pair[0], right_pair[1]) + matmul_high(left_pair[1], right_pair[0])
    return (real_part, imag_part)


def real_left(matrix, pair_value):
    return (matmul_high(matrix, pair_value[0]), matmul_high(matrix, pair_value[1]))


def real_right(pair_value, matrix):
    return (matmul_high(pair_value[0], matrix), matmul_high(pair_value[1], matrix))


def adjoint(pair_value):
    return (jnp.swapaxes(pair_value[0], -1, -2), -jnp.swapaxes(pair_value[1], -1, -2))


def add_pair(left_pair, right_pair):
    return (left_pair[0] + right_pair[0], left_pair[1] + right_pair[1])


def sub_pair(left_pair, right_pair):
    return (left_pair[0] - right_pair[0], left_pair[1] - right_pair[1])


def sweep_kernel(normal_re_ref, normal_im_ref, out_re_ref, out_im_ref):
    batch, orbitals, _ = normal_re_ref.shape
    out_re_ref[...] = normal_re_ref[...]
    out_im_ref[...] = normal_im_ref[...]
    lane = lax.broadcasted_iota(jnp.int32, (1, orbitals), 1)
    row_index = lax.broadcasted_iota(jnp.int32, (orbitals, 1), 0)

    def step(pivot, carry):
        lane_hit = lane == pivot
        row_hit = row_index == pivot
        for item in range(batch):
            whole_re = out_re_ref[item]
            whole_im = out_im_ref[item]
            row_re = out_re_ref[item, pl.ds(pivot, 1), :]
            row_im = out_im_ref[item, pl.ds(pivot, 1), :]
            col_re = jnp.sum(jnp.where(lane_hit, whole_re, 0.0), axis=1, keepdims=True)
            col_im = jnp.sum(jnp.where(lane_hit, whole_im, 0.0), axis=1, keepdims=True)
            piv_re = jnp.sum(jnp.where(lane_hit, row_re, 0.0), axis=1, keepdims=True)
            piv_im = jnp.sum(jnp.where(lane_hit, row_im, 0.0), axis=1, keepdims=True)
            norm = piv_re * piv_re + piv_im * piv_im
            inv_re = piv_re / norm
            inv_im = -piv_im / norm
            scaled_re = jnp.where(lane_hit, inv_re, row_re * inv_re - row_im * inv_im)
            scaled_im = jnp.where(lane_hit, inv_im, row_re * inv_im + row_im * inv_re)
            col_re = jnp.where(row_hit, 0.0, col_re)
            col_im = jnp.where(row_hit, 0.0, col_im)
            base_re = jnp.where(lane_hit, 0.0, whole_re)
            base_im = jnp.where(lane_hit, 0.0, whole_im)
            out_re_ref[item] = base_re - (col_re * scaled_re - col_im * scaled_im)
            out_im_ref[item] = base_im - (col_re * scaled_im + col_im * scaled_re)
            out_re_ref[item, pl.ds(pivot, 1), :] = scaled_re
            out_im_ref[item, pl.ds(pivot, 1), :] = scaled_im
        return carry

    lax.fori_loop(0, orbitals, step, 0)


def hermitian_inverse(normal_pair, interpret=False):
    shape = normal_pair[0].shape
    orbitals = shape[-1]
    flat = [item.reshape(-1, orbitals, orbitals) for item in normal_pair]
    out_shape = jax.ShapeDtypeStruct(flat[0].shape, jnp.float32)
    inverse = pl.pallas_call(
        sweep_kernel,
        out_shape=(out_shape, out_shape),
        interpret=interpret,
    )(*flat)
    return (inverse[0].reshape(shape), inverse[1].reshape(shape))


def invert_pair(pair_value, interpret=False):
    adjoint_value = adjoint(pair_value)
    normal = complex_product(adjoint_value, pair_value)
    normal_inverse = hermitian_inverse(normal, interpret)
    return complex_product(normal_inverse, adjoint_value)


def greater_of(less_pair, ret_pair):
    return sub_pair(add_pair(less_pair, ret_pair), adjoint(ret_pair))


def pack_pair(pair_value):
    return jnp.stack([pair_value[0], pair_value[1]], axis=-3)


def green_blocks(sigma_less, sigma_great, hamilton, slab_coupling, energies, fence=None):
    orbitals = sigma_less.shape[-1]
    slab_count = sigma_less.shape[2]
    identity = jnp.eye(orbitals, dtype=jnp.float32)
    energy_grid = energies[None, :, None, None]
    left_ret = []
    left_less = []
    for slab_index in range(slab_count):
        lesser = sigma_less[:, :, slab_index].astype(jnp.float32)
        greater = sigma_great[:, :, slab_index].astype(jnp.float32)
        retarded_re = 0.5 * (greater[:, :, 0] - lesser[:, :, 0])
        retarded_im = 0.5 * (greater[:, :, 1] - lesser[:, :, 1]) - DAMPING * identity
        system_re = energy_grid * identity - hamilton[:, :, slab_index] - retarded_re
        system_im = -retarded_im
        source = (lesser[:, :, 0], lesser[:, :, 1])
        if fence is not None and slab_index == slab_count - 1:
            fence, system_re, system_im = lax.optimization_barrier((fence, system_re, system_im))
        if slab_index > 0:
            coupling = slab_coupling[slab_index - 1]
            folded = real_right(real_left(coupling, left_ret[-1]), coupling.T)
            system_re = system_re - folded[0]
            system_im = system_im - folded[1]
            source = add_pair(source, real_right(real_left(coupling, left_less[-1]), coupling.T))
        inverse = invert_pair((system_re, system_im))
        left_ret.append(inverse)
        left_less.append(complex_product(complex_product(inverse, source), adjoint(inverse)))
    full_ret = left_ret[-1]
    full_less = left_less[-1]
    lesser_list = [full_less]
    greater_list = [greater_of(full_less, full_ret)]
    for slab_index in range(slab_count - 2, -1, -1):
        coupling = slab_coupling[slab_index]
        green_couple = real_right(left_ret[slab_index], coupling)
        bridge = real_right(complex_product(green_couple, full_ret), coupling.T)
        cross_term = complex_product(bridge, left_less[slab_index])
        spread = complex_product(
            real_right(complex_product(green_couple, full_less), coupling.T),
            adjoint(left_ret[slab_index]),
        )
        full_less = add_pair(
            add_pair(left_less[slab_index], spread), sub_pair(cross_term, adjoint(cross_term))
        )
        full_ret = add_pair(left_ret[slab_index], complex_product(bridge, left_ret[slab_index]))
        lesser_list.insert(0, full_less)
        greater_list.insert(0, greater_of(full_less, full_ret))
    finished = [
        jnp.stack([pack_pair(less_item), pack_pair(great_item)], axis=2).astype(jnp.bfloat16)
        for less_item, great_item in zip(lesser_list, greater_list)
    ]
    return finished, fence


def hamiltonian(onsite_table, cos_coupling, slab_kind, momenta_index, momenta_total):
    kind_count = onsite_table.shape[0]
    choose = (slab_kind[:, None] == jnp.arange(kind_count, dtype=jnp.int32)[None, :]).astype(
        jnp.float32
    )
    onsite = jnp.einsum("sk,kij->sij", choose, onsite_table, precision=lax.Precision.HIGHEST)
    phase_factor = jnp.cos(2.0 * jnp.pi * momenta_index.astype(jnp.float32) / momenta_total)
    hamilton = onsite[None] + phase_factor[:, None, None, None] * cos_coupling[None]
    return hamilton[:, None]


def momentum_weights(table_rows, mode_weight, momenta_total):
    onehot = (
        table_rows[:, :, None] == jnp.arange(momenta_total, dtype=jnp.int32)[None, None, :]
    ).astype(jnp.float32)
    return (
        jnp.einsum("lq,aqk->lak", mode_weight, onehot, precision=lax.Precision.HIGHEST)
        / momenta_total
    )


def mixed_sums(extended, weights, form_factor, occupation, energy_offset, energy_count, margin):
    total_less = None
    total_great = None
    for mode_index in range(form_factor.shape[0]):
        shift_steps = energy_offset[mode_index]
        upper_side = lax.dynamic_slice_in_dim(extended, margin + shift_steps, energy_count, 1)
        lower_side = lax.dynamic_slice_in_dim(extended, margin - shift_steps, energy_count, 1)
        occupied = occupation[mode_index]
        less_term = (occupied + 1.0) * upper_side[:, :, 0].astype(
            jnp.float32
        ) + occupied * lower_side[:, :, 0].astype(jnp.float32)
        great_term = (occupied + 1.0) * lower_side[:, :, 1].astype(
            jnp.float32
        ) + occupied * upper_side[:, :, 1].astype(jnp.float32)
        mode_weights = weights[mode_index].reshape(
            weights.shape[1:] + (1,) * (less_term.ndim - 1)
        )
        less_sum = form_factor[mode_index] * jnp.sum(mode_weights * less_term[None], axis=1)
        great_sum = form_factor[mode_index] * jnp.sum(mode_weights * great_term[None], axis=1)
        total_less = less_sum if total_less is None else total_less + less_sum
        total_great = great_sum if total_great is None else total_great + great_sum
    return (total_less, total_great)


def exchange_blocks(blocks, width):
    count = lax.axis_size("kz")
    far_pairs = [(i, (i + 2) % count) for i in range(count)]
    near_pairs = [(i, i ^ 1) for i in range(count)]
    far = lax.ppermute(blocks, "kz", far_pairs)
    own_extended = padded(blocks, (("en", 1),), width)
    far_extended = padded(far, (("en", 1),), width)
    extended = jnp.concatenate([own_extended, far_extended], axis=0)
    other = lax.ppermute(extended, "kz", near_pairs)
    everyone = jnp.concatenate([extended, other], axis=0)
    return tuple(
        lax.slice_in_dim(everyone, index * width, (index + 1) * width, axis=1)
        for index in range(3)
    )


def arrival_order():
    count = lax.axis_size("kz")
    momentum = lax.axis_index("kz")
    partner = momentum ^ 1
    return jnp.stack([momentum, (momentum + 2) % count, partner, (partner + 2) % count])


def on_device(
    sigma_less,
    sigma_great,
    onsite_table,
    cos_coupling,
    slab_coupling,
    slab_kind,
    kz_table,
    mode_weight,
    form_factor,
    occupation,
    energy_offset,
):
    momenta_local = sigma_less.shape[0]
    energy_local = sigma_less.shape[1]
    momenta_total = momenta_local * lax.axis_size("kz")
    energy_total = energy_local * lax.axis_size("en")
    momenta_start = lax.axis_index("kz") * momenta_local
    momenta_index = momenta_start + jnp.arange(momenta_local, dtype=jnp.int32)
    energy_index = lax.axis_index("en") * energy_local + jnp.arange(energy_local, dtype=jnp.int32)
    energies = -1.5 + 3.0 * (energy_index.astype(jnp.float32) + 0.5) / energy_total
    hamilton = hamiltonian(onsite_table, cos_coupling, slab_kind, momenta_index, momenta_total)
    chunk_count = 2 if energy_local % 2 == 0 else 1
    chunk = energy_local // chunk_count
    table_rows = lax.dynamic_slice_in_dim(kz_table, momenta_start, momenta_local, 0)
    weights = momentum_weights(table_rows, mode_weight, momenta_total)
    weights = jnp.take(weights, arrival_order(), axis=2)
    pieces = []
    previous = None
    for chunk_index in range(chunk_count):
        window = slice(chunk_index * chunk, (chunk_index + 1) * chunk)
        chunk_inputs = (sigma_less[:, window], sigma_great[:, window], energies[window])
        if previous is not None:
            previous, chunk_inputs = lax.optimization_barrier((previous, chunk_inputs))
        slab_blocks, fenced = green_blocks(
            chunk_inputs[0],
            chunk_inputs[1],
            hamilton,
            slab_coupling,
            chunk_inputs[2],
            pieces if pieces else None,
        )
        if fenced is not None:
            pieces = fenced
        previous = slab_blocks
        pieces = pieces + [[exchange_blocks(blocks, chunk) for blocks in slab_blocks]]
    less_parts = []
    great_parts = []
    for slab_index in range(len(pieces[0])):
        extended = jnp.concatenate(
            [
                chunk_pieces[slab_index][side]
                for side in range(3)
                for chunk_pieces in pieces
            ],
            axis=1,
        )
        less_part, great_part = mixed_sums(
            extended, weights, form_factor, occupation, energy_offset, energy_local, energy_local
        )
        less_parts.append(less_part.astype(jnp.bfloat16))
        great_parts.append(great_part.astype(jnp.bfloat16))
    return (jnp.stack(less_parts, axis=2), jnp.stack(great_parts, axis=2))


def solution(mesh):
    in_specs = (
        P("kz", "en", None, None, None, None),
        P("kz", "en", None, None, None, None),
        P(),
        P(),
        P(),
        P(),
        P(),
        P(),
        P(),
        P(),
        P(),
    )
    out_specs = (P("kz", "en", None, None, None, None), P("kz", "en", None, None, None, None))
    return jax.shard_map(
        on_device, mesh=mesh, in_specs=in_specs, out_specs=out_specs, check_vma=False
    )
```

```python
import jax
import jax.numpy as jnp
from jax import lax
from jax.sharding import PartitionSpec as P
from jax.experimental import pallas as pl

OFFMAX = 4


DAMPING = 0.3


def padded(block, sides, width):
    for axis, dim in sides:
        count = lax.axis_size(axis)
        forward = [(i, i + 1) for i in range(count - 1)]
        backward = [(target, source) for source, target in forward]
        low = lax.ppermute(
            lax.slice_in_dim(block, block.shape[dim] - width, None, axis=dim), axis, forward
        )
        high = lax.ppermute(lax.slice_in_dim(block, 0, width, axis=dim), axis, backward)
        block = jnp.concatenate([low, block, high], axis=dim)
    return block


def matmul_high(left_matrix, right_matrix):
    return jnp.matmul(left_matrix, right_matrix, precision=lax.Precision.HIGHEST)


def complex_product(left_pair, right_pair):
    real_part = matmul_high(left_pair[0], right_pair[0]) - matmul_high(left_pair[1], right_pair[1])
    imag_part = matmul_high(left_pair[0], right_pair[1]) + matmul_high(left_pair[1], right_pair[0])
    return (real_part, imag_part)


def real_left(matrix, pair_value):
    return (matmul_high(matrix, pair_value[0]), matmul_high(matrix, pair_value[1]))


def real_right(pair_value, matrix):
    return (matmul_high(pair_value[0], matrix), matmul_high(pair_value[1], matrix))


def adjoint(pair_value):
    return (jnp.swapaxes(pair_value[0], -1, -2), -jnp.swapaxes(pair_value[1], -1, -2))


def add_pair(left_pair, right_pair):
    return (left_pair[0] + right_pair[0], left_pair[1] + right_pair[1])


def sub_pair(left_pair, right_pair):
    return (left_pair[0] - right_pair[0], left_pair[1] - right_pair[1])


def sweep_kernel(normal_re_ref, normal_im_ref, out_re_ref, out_im_ref):
    batch, orbitals, _ = normal_re_ref.shape
    out_re_ref[...] = normal_re_ref[...]
    out_im_ref[...] = normal_im_ref[...]
    lane = lax.broadcasted_iota(jnp.int32, (1, orbitals), 1)
    row_index = lax.broadcasted_iota(jnp.int32, (orbitals, 1), 0)

    def step(pivot, carry):
        lane_hit = lane == pivot
        row_hit = row_index == pivot
        for item in range(batch):
            whole_re = out_re_ref[item]
            whole_im = out_im_ref[item]
            row_re = out_re_ref[item, pl.ds(pivot, 1), :]
            row_im = out_im_ref[item, pl.ds(pivot, 1), :]
            col_re = jnp.sum(jnp.where(lane_hit, whole_re, 0.0), axis=1, keepdims=True)
            col_im = jnp.sum(jnp.where(lane_hit, whole_im, 0.0), axis=1, keepdims=True)
            piv_re = jnp.sum(jnp.where(lane_hit, row_re, 0.0), axis=1, keepdims=True)
            piv_im = jnp.sum(jnp.where(lane_hit, row_im, 0.0), axis=1, keepdims=True)
            norm = piv_re * piv_re + piv_im * piv_im
            inv_re = piv_re / norm
            inv_im = -piv_im / norm
            scaled_re = jnp.where(lane_hit, inv_re, row_re * inv_re - row_im * inv_im)
            scaled_im = jnp.where(lane_hit, inv_im, row_re * inv_im + row_im * inv_re)
            col_re = jnp.where(row_hit, 0.0, col_re)
            col_im = jnp.where(row_hit, 0.0, col_im)
            base_re = jnp.where(lane_hit, 0.0, whole_re)
            base_im = jnp.where(lane_hit, 0.0, whole_im)
            out_re_ref[item] = base_re - (col_re * scaled_re - col_im * scaled_im)
            out_im_ref[item] = base_im - (col_re * scaled_im + col_im * scaled_re)
            out_re_ref[item, pl.ds(pivot, 1), :] = scaled_re
            out_im_ref[item, pl.ds(pivot, 1), :] = scaled_im
        return carry

    lax.fori_loop(0, orbitals, step, 0)


def hermitian_inverse(normal_pair, interpret=False):
    shape = normal_pair[0].shape
    orbitals = shape[-1]
    flat = [item.reshape(-1, orbitals, orbitals) for item in normal_pair]
    out_shape = jax.ShapeDtypeStruct(flat[0].shape, jnp.float32)
    inverse = pl.pallas_call(
        sweep_kernel,
        out_shape=(out_shape, out_shape),
        interpret=interpret,
    )(*flat)
    return (inverse[0].reshape(shape), inverse[1].reshape(shape))


def invert_pair(pair_value, interpret=False):
    adjoint_value = adjoint(pair_value)
    normal = complex_product(adjoint_value, pair_value)
    normal_inverse = hermitian_inverse(normal, interpret)
    return complex_product(normal_inverse, adjoint_value)


def greater_of(less_pair, ret_pair):
    return sub_pair(add_pair(less_pair, ret_pair), adjoint(ret_pair))


def pack_pair(pair_value):
    return jnp.stack([pair_value[0], pair_value[1]], axis=-3)


def green_blocks(sigma_less, sigma_great, hamilton, slab_coupling, energies):
    orbitals = sigma_less.shape[-1]
    slab_count = sigma_less.shape[2]
    identity = jnp.eye(orbitals, dtype=jnp.float32)
    energy_grid = energies[None, :, None, None]
    left_ret = []
    left_less = []
    for slab_index in range(slab_count):
        lesser = sigma_less[:, :, slab_index].astype(jnp.float32)
        greater = sigma_great[:, :, slab_index].astype(jnp.float32)
        retarded_re = 0.5 * (greater[:, :, 0] - lesser[:, :, 0])
        retarded_im = 0.5 * (greater[:, :, 1] - lesser[:, :, 1]) - DAMPING * identity
        system_re = energy_grid * identity - hamilton[:, :, slab_index] - retarded_re
        system_im = -retarded_im
        source = (lesser[:, :, 0], lesser[:, :, 1])
        if slab_index > 0:
            coupling = slab_coupling[slab_index - 1]
            folded = real_right(real_left(coupling, left_ret[-1]), coupling.T)
            system_re = system_re - folded[0]
            system_im = system_im - folded[1]
            source = add_pair(source, real_right(real_left(coupling, left_less[-1]), coupling.T))
        inverse = invert_pair((system_re, system_im))
        left_ret.append(inverse)
        left_less.append(complex_product(complex_product(inverse, source), adjoint(inverse)))
    full_ret = left_ret[-1]
    full_less = left_less[-1]
    lesser_list = [full_less]
    greater_list = [greater_of(full_less, full_ret)]
    for slab_index in range(slab_count - 2, -1, -1):
        coupling = slab_coupling[slab_index]
        green_couple = real_right(left_ret[slab_index], coupling)
        bridge = real_right(complex_product(green_couple, full_ret), coupling.T)
        cross_term = complex_product(bridge, left_less[slab_index])
        spread = complex_product(
            real_right(complex_product(green_couple, full_less), coupling.T),
            adjoint(left_ret[slab_index]),
        )
        full_less = add_pair(
            add_pair(left_less[slab_index], spread), sub_pair(cross_term, adjoint(cross_term))
        )
        full_ret = add_pair(left_ret[slab_index], complex_product(bridge, left_ret[slab_index]))
        lesser_list.insert(0, full_less)
        greater_list.insert(0, greater_of(full_less, full_ret))
    return [
        jnp.stack([pack_pair(less_item), pack_pair(great_item)], axis=2).astype(jnp.bfloat16)
        for less_item, great_item in zip(lesser_list, greater_list)
    ]


def hamiltonian(onsite_table, cos_coupling, slab_kind, momenta_index, momenta_total):
    kind_count = onsite_table.shape[0]
    choose = (slab_kind[:, None] == jnp.arange(kind_count, dtype=jnp.int32)[None, :]).astype(
        jnp.float32
    )
    onsite = jnp.einsum("sk,kij->sij", choose, onsite_table, precision=lax.Precision.HIGHEST)
    phase_factor = jnp.cos(2.0 * jnp.pi * momenta_index.astype(jnp.float32) / momenta_total)
    hamilton = onsite[None] + phase_factor[:, None, None, None] * cos_coupling[None]
    return hamilton[:, None]


def momentum_weights(table_rows, mode_weight, momenta_total):
    onehot = (
        table_rows[:, :, None] == jnp.arange(momenta_total, dtype=jnp.int32)[None, None, :]
    ).astype(jnp.float32)
    return (
        jnp.einsum("lq,aqk->lak", mode_weight, onehot, precision=lax.Precision.HIGHEST)
        / momenta_total
    )


def mixed_sums(extended, weights, form_factor, occupation, energy_offset, energy_count, margin):
    total_less = None
    total_great = None
    for mode_index in range(form_factor.shape[0]):
        shift_steps = energy_offset[mode_index]
        upper_side = lax.dynamic_slice_in_dim(extended, margin + shift_steps, energy_count, 1)
        lower_side = lax.dynamic_slice_in_dim(extended, margin - shift_steps, energy_count, 1)
        occupied = occupation[mode_index]
        less_term = (occupied + 1.0) * upper_side[:, :, 0].astype(
            jnp.float32
        ) + occupied * lower_side[:, :, 0].astype(jnp.float32)
        great_term = (occupied + 1.0) * lower_side[:, :, 1].astype(
            jnp.float32
        ) + occupied * upper_side[:, :, 1].astype(jnp.float32)
        mode_weights = weights[mode_index].reshape(
            weights.shape[1:] + (1,) * (less_term.ndim - 1)
        )
        less_sum = form_factor[mode_index] * jnp.sum(mode_weights * less_term[None], axis=1)
        great_sum = form_factor[mode_index] * jnp.sum(mode_weights * great_term[None], axis=1)
        total_less = less_sum if total_less is None else total_less + less_sum
        total_great = great_sum if total_great is None else total_great + great_sum
    return (total_less, total_great)


def exchange_blocks(blocks, width):
    count = lax.axis_size("kz")
    lanes = lax.axis_size("en")
    momentum = lax.axis_index("kz")

    def far_of(index):
        return (index + 2) % count

    def joint(index, lane):
        return index * lanes + lane

    near_pairs = [(i, i ^ 1) for i in range(count)]
    far = lax.ppermute(blocks, "kz", [(i, far_of(i)) for i in range(count)])
    tail = lax.slice_in_dim(blocks, blocks.shape[1] - width, None, axis=1)
    head = lax.slice_in_dim(blocks, 0, width, axis=1)
    forward = [(lane, lane + 1) for lane in range(lanes - 1)]
    backward = [(lane + 1, lane) for lane in range(lanes - 1)]
    low_same = lax.ppermute(tail, "en", forward)
    high_same = lax.ppermute(head, "en", backward)
    low_far = lax.ppermute(
        tail,
        ("kz", "en"),
        [(joint(far_of(i), lane), joint(i, lane + 1)) for i in range(count) for lane in range(lanes - 1)],
    )
    high_far = lax.ppermute(
        head,
        ("kz", "en"),
        [(joint(far_of(i), lane + 1), joint(i, lane)) for i in range(count) for lane in range(lanes - 1)],
    )
    own_extended = jnp.concatenate([low_same, blocks, high_same], axis=1)
    far_extended = jnp.concatenate([low_far, far, high_far], axis=1)
    extended = jnp.concatenate([own_extended, far_extended], axis=0)
    other = lax.ppermute(extended, "kz", near_pairs)
    everyone = jnp.concatenate([extended, other], axis=0)
    partner = momentum ^ 1
    order = jnp.stack([momentum, far_of(momentum), partner, far_of(partner)])
    return everyone, order


def on_device(
    sigma_less,
    sigma_great,
    onsite_table,
    cos_coupling,
    slab_coupling,
    slab_kind,
    kz_table,
    mode_weight,
    form_factor,
    occupation,
    energy_offset,
):
    momenta_local = sigma_less.shape[0]
    energy_local = sigma_less.shape[1]
    momenta_total = momenta_local * lax.axis_size("kz")
    energy_total = energy_local * lax.axis_size("en")
    momenta_start = lax.axis_index("kz") * momenta_local
    momenta_index = momenta_start + jnp.arange(momenta_local, dtype=jnp.int32)
    energy_index = lax.axis_index("en") * energy_local + jnp.arange(energy_local, dtype=jnp.int32)
    energies = -1.5 + 3.0 * (energy_index.astype(jnp.float32) + 0.5) / energy_total
    hamilton = hamiltonian(onsite_table, cos_coupling, slab_kind, momenta_index, momenta_total)
    slab_blocks = green_blocks(sigma_less, sigma_great, hamilton, slab_coupling, energies)
    table_rows = lax.dynamic_slice_in_dim(kz_table, momenta_start, momenta_local, 0)
    weights = momentum_weights(table_rows, mode_weight, momenta_total)
    less_parts = []
    great_parts = []
    for blocks in slab_blocks:
        extended, order = exchange_blocks(blocks, OFFMAX)
        less_part, great_part = mixed_sums(
            extended,
            jnp.take(weights, order, axis=2),
            form_factor,
            occupation,
            energy_offset,
            energy_local,
            OFFMAX,
        )
        less_parts.append(less_part.astype(jnp.bfloat16))
        great_parts.append(great_part.astype(jnp.bfloat16))
    return (jnp.stack(less_parts, axis=2), jnp.stack(great_parts, axis=2))


def solution(mesh):
    in_specs = (
        P("kz", "en", None, None, None, None),
        P("kz", "en", None, None, None, None),
        P(),
        P(),
        P(),
        P(),
        P(),
        P(),
        P(),
        P(),
        P(),
    )
    out_specs = (P("kz", "en", None, None, None, None), P("kz", "en", None, None, None, None))
    return jax.shard_map(
        on_device, mesh=mesh, in_specs=in_specs, out_specs=out_specs, check_vma=False
    )
```

```python
import jax
import jax.numpy as jnp
from jax import lax
from jax.sharding import PartitionSpec as P
from jax.experimental import pallas as pl

OFFMAX = 4


DAMPING = 0.3


def padded(block, sides, width):
    for axis, dim in sides:
        count = lax.axis_size(axis)
        forward = [(i, i + 1) for i in range(count - 1)]
        backward = [(target, source) for source, target in forward]
        low = lax.ppermute(
            lax.slice_in_dim(block, block.shape[dim] - width, None, axis=dim), axis, forward
        )
        high = lax.ppermute(lax.slice_in_dim(block, 0, width, axis=dim), axis, backward)
        block = jnp.concatenate([low, block, high], axis=dim)
    return block


def matmul_high(left_matrix, right_matrix):
    return jnp.matmul(left_matrix, right_matrix, precision=lax.Precision.HIGHEST)


def complex_product(left_pair, right_pair):
    real_part = matmul_high(left_pair[0], right_pair[0]) - matmul_high(left_pair[1], right_pair[1])
    imag_part = matmul_high(left_pair[0], right_pair[1]) + matmul_high(left_pair[1], right_pair[0])
    return (real_part, imag_part)


def real_left(matrix, pair_value):
    return (matmul_high(matrix, pair_value[0]), matmul_high(matrix, pair_value[1]))


def real_right(pair_value, matrix):
    return (matmul_high(pair_value[0], matrix), matmul_high(pair_value[1], matrix))


def adjoint(pair_value):
    return (jnp.swapaxes(pair_value[0], -1, -2), -jnp.swapaxes(pair_value[1], -1, -2))


def add_pair(left_pair, right_pair):
    return (left_pair[0] + right_pair[0], left_pair[1] + right_pair[1])


def sub_pair(left_pair, right_pair):
    return (left_pair[0] - right_pair[0], left_pair[1] - right_pair[1])


def sweep_kernel(normal_re_ref, normal_im_ref, out_re_ref, out_im_ref):
    batch, orbitals, _ = normal_re_ref.shape
    out_re_ref[...] = normal_re_ref[...]
    out_im_ref[...] = normal_im_ref[...]
    lane = lax.broadcasted_iota(jnp.int32, (1, orbitals), 1)
    row_index = lax.broadcasted_iota(jnp.int32, (orbitals, 1), 0)

    def step(pivot, carry):
        lane_hit = lane == pivot
        row_hit = row_index == pivot
        for item in range(batch):
            whole_re = out_re_ref[item]
            whole_im = out_im_ref[item]
            row_re = out_re_ref[item, pl.ds(pivot, 1), :]
            row_im = out_im_ref[item, pl.ds(pivot, 1), :]
            col_re = jnp.sum(jnp.where(lane_hit, whole_re, 0.0), axis=1, keepdims=True)
            col_im = jnp.sum(jnp.where(lane_hit, whole_im, 0.0), axis=1, keepdims=True)
            piv_re = jnp.sum(jnp.where(lane_hit, row_re, 0.0), axis=1, keepdims=True)
            piv_im = jnp.sum(jnp.where(lane_hit, row_im, 0.0), axis=1, keepdims=True)
            norm = piv_re * piv_re + piv_im * piv_im
            inv_re = piv_re / norm
            inv_im = -piv_im / norm
            scaled_re = jnp.where(lane_hit, inv_re, row_re * inv_re - row_im * inv_im)
            scaled_im = jnp.where(lane_hit, inv_im, row_re * inv_im + row_im * inv_re)
            col_re = jnp.where(row_hit, 0.0, col_re)
            col_im = jnp.where(row_hit, 0.0, col_im)
            base_re = jnp.where(lane_hit, 0.0, whole_re)
            base_im = jnp.where(lane_hit, 0.0, whole_im)
            out_re_ref[item] = base_re - (col_re * scaled_re - col_im * scaled_im)
            out_im_ref[item] = base_im - (col_re * scaled_im + col_im * scaled_re)
            out_re_ref[item, pl.ds(pivot, 1), :] = scaled_re
            out_im_ref[item, pl.ds(pivot, 1), :] = scaled_im
        return carry

    lax.fori_loop(0, orbitals, step, 0)


def hermitian_inverse(normal_pair, interpret=False):
    shape = normal_pair[0].shape
    orbitals = shape[-1]
    flat = [item.reshape(-1, orbitals, orbitals) for item in normal_pair]
    out_shape = jax.ShapeDtypeStruct(flat[0].shape, jnp.float32)
    inverse = pl.pallas_call(
        sweep_kernel,
        out_shape=(out_shape, out_shape),
        interpret=interpret,
    )(*flat)
    return (inverse[0].reshape(shape), inverse[1].reshape(shape))


def invert_pair(pair_value, interpret=False):
    adjoint_value = adjoint(pair_value)
    normal = complex_product(adjoint_value, pair_value)
    normal_inverse = hermitian_inverse(normal, interpret)
    return complex_product(normal_inverse, adjoint_value)


def greater_of(less_pair, ret_pair):
    return sub_pair(add_pair(less_pair, ret_pair), adjoint(ret_pair))


def pack_pair(pair_value):
    return jnp.stack([pair_value[0], pair_value[1]], axis=-3)


def green_blocks(sigma_less, sigma_great, hamilton, slab_coupling, energies):
    orbitals = sigma_less.shape[-1]
    slab_count = sigma_less.shape[2]
    identity = jnp.eye(orbitals, dtype=jnp.float32)
    energy_grid = energies[None, :, None, None]
    left_ret = []
    left_less = []
    for slab_index in range(slab_count):
        lesser = sigma_less[:, :, slab_index].astype(jnp.float32)
        greater = sigma_great[:, :, slab_index].astype(jnp.float32)
        retarded_re = 0.5 * (greater[:, :, 0] - lesser[:, :, 0])
        retarded_im = 0.5 * (greater[:, :, 1] - lesser[:, :, 1]) - DAMPING * identity
        system_re = energy_grid * identity - hamilton[:, :, slab_index] - retarded_re
        system_im = -retarded_im
        source = (lesser[:, :, 0], lesser[:, :, 1])
        if slab_index > 0:
            coupling = slab_coupling[slab_index - 1]
            folded = real_right(real_left(coupling, left_ret[-1]), coupling.T)
            system_re = system_re - folded[0]
            system_im = system_im - folded[1]
            source = add_pair(source, real_right(real_left(coupling, left_less[-1]), coupling.T))
        inverse = invert_pair((system_re, system_im))
        left_ret.append(inverse)
        left_less.append(complex_product(complex_product(inverse, source), adjoint(inverse)))
    full_ret = left_ret[-1]
    full_less = left_less[-1]
    lesser_list = [full_less]
    greater_list = [greater_of(full_less, full_ret)]
    for slab_index in range(slab_count - 2, -1, -1):
        coupling = slab_coupling[slab_index]
        green_couple = real_right(left_ret[slab_index], coupling)
        bridge = real_right(complex_product(green_couple, full_ret), coupling.T)
        cross_term = complex_product(bridge, left_less[slab_index])
        spread = complex_product(
            real_right(complex_product(green_couple, full_less), coupling.T),
            adjoint(left_ret[slab_index]),
        )
        full_less = add_pair(
            add_pair(left_less[slab_index], spread), sub_pair(cross_term, adjoint(cross_term))
        )
        full_ret = add_pair(left_ret[slab_index], complex_product(bridge, left_ret[slab_index]))
        lesser_list.insert(0, full_less)
        greater_list.insert(0, greater_of(full_less, full_ret))
    return [
        jnp.stack([pack_pair(less_item), pack_pair(great_item)], axis=2).astype(jnp.bfloat16)
        for less_item, great_item in zip(lesser_list, greater_list)
    ]


def hamiltonian(onsite_table, cos_coupling, slab_kind, momenta_index, momenta_total):
    kind_count = onsite_table.shape[0]
    choose = (slab_kind[:, None] == jnp.arange(kind_count, dtype=jnp.int32)[None, :]).astype(
        jnp.float32
    )
    onsite = jnp.einsum("sk,kij->sij", choose, onsite_table, precision=lax.Precision.HIGHEST)
    phase_factor = jnp.cos(2.0 * jnp.pi * momenta_index.astype(jnp.float32) / momenta_total)
    hamilton = onsite[None] + phase_factor[:, None, None, None] * cos_coupling[None]
    return hamilton[:, None]


def momentum_weights(table_rows, mode_weight, momenta_total):
    onehot = (
        table_rows[:, :, None] == jnp.arange(momenta_total, dtype=jnp.int32)[None, None, :]
    ).astype(jnp.float32)
    return (
        jnp.einsum("lq,aqk->lak", mode_weight, onehot, precision=lax.Precision.HIGHEST)
        / momenta_total
    )


def mixed_sums(extended, weights, form_factor, occupation, energy_offset, energy_count, margin):
    total_less = None
    total_great = None
    for mode_index in range(form_factor.shape[0]):
        shift_steps = energy_offset[mode_index]
        upper_side = lax.dynamic_slice_in_dim(extended, margin + shift_steps, energy_count, 1)
        lower_side = lax.dynamic_slice_in_dim(extended, margin - shift_steps, energy_count, 1)
        occupied = occupation[mode_index]
        less_term = (occupied + 1.0) * upper_side[:, :, 0].astype(
            jnp.float32
        ) + occupied * lower_side[:, :, 0].astype(jnp.float32)
        great_term = (occupied + 1.0) * lower_side[:, :, 1].astype(
            jnp.float32
        ) + occupied * upper_side[:, :, 1].astype(jnp.float32)
        mode_weights = weights[mode_index].reshape(
            weights.shape[1:] + (1,) * (less_term.ndim - 1)
        )
        less_sum = form_factor[mode_index] * jnp.sum(mode_weights * less_term[None], axis=1)
        great_sum = form_factor[mode_index] * jnp.sum(mode_weights * great_term[None], axis=1)
        total_less = less_sum if total_less is None else total_less + less_sum
        total_great = great_sum if total_great is None else total_great + great_sum
    return (total_less, total_great)


def exchange_blocks(blocks, width):
    count = lax.axis_size("kz")
    lanes = lax.axis_size("en")

    def far_of(index):
        return (index + 2) % count

    def joint(index, lane):
        return index * lanes + lane

    far = lax.ppermute(blocks, "kz", [(i, far_of(i)) for i in range(count)])
    tail = lax.slice_in_dim(blocks, blocks.shape[1] - width, None, axis=1)
    head = lax.slice_in_dim(blocks, 0, width, axis=1)
    forward = [(lane, lane + 1) for lane in range(lanes - 1)]
    backward = [(lane + 1, lane) for lane in range(lanes - 1)]
    low_same = lax.ppermute(tail, "en", forward)
    high_same = lax.ppermute(head, "en", backward)
    low_far = lax.ppermute(
        tail,
        ("kz", "en"),
        [(joint(far_of(i), lane), joint(i, lane + 1)) for i in range(count) for lane in range(lanes - 1)],
    )
    high_far = lax.ppermute(
        head,
        ("kz", "en"),
        [(joint(far_of(i), lane + 1), joint(i, lane)) for i in range(count) for lane in range(lanes - 1)],
    )
    own_extended = jnp.concatenate([low_same, blocks, high_same], axis=1)
    far_extended = jnp.concatenate([low_far, far, high_far], axis=1)
    return jnp.concatenate([own_extended, far_extended], axis=0)


def on_device(
    sigma_less,
    sigma_great,
    onsite_table,
    cos_coupling,
    slab_coupling,
    slab_kind,
    kz_table,
    mode_weight,
    form_factor,
    occupation,
    energy_offset,
):
    momenta_local = sigma_less.shape[0]
    energy_local = sigma_less.shape[1]
    momenta_total = momenta_local * lax.axis_size("kz")
    energy_total = energy_local * lax.axis_size("en")
    momenta_start = lax.axis_index("kz") * momenta_local
    momenta_index = momenta_start + jnp.arange(momenta_local, dtype=jnp.int32)
    energy_index = lax.axis_index("en") * energy_local + jnp.arange(energy_local, dtype=jnp.int32)
    energies = -1.5 + 3.0 * (energy_index.astype(jnp.float32) + 0.5) / energy_total
    hamilton = hamiltonian(onsite_table, cos_coupling, slab_kind, momenta_index, momenta_total)
    slab_blocks = green_blocks(sigma_less, sigma_great, hamilton, slab_coupling, energies)
    count = lax.axis_size("kz")
    momentum = lax.axis_index("kz")
    partner = momentum ^ 1
    held = jnp.stack([momentum, (momentum + 2) % count])
    all_weights = momentum_weights(kz_table, mode_weight, momenta_total)
    own_weights = jnp.take(jnp.take(all_weights, momentum[None], axis=1), held, axis=2)
    partner_weights = jnp.take(jnp.take(all_weights, partner[None], axis=1), held, axis=2)
    near_pairs = [(i, i ^ 1) for i in range(count)]
    less_parts = []
    great_parts = []
    for blocks in slab_blocks:
        extended = exchange_blocks(blocks, OFFMAX)
        settings = (form_factor, occupation, energy_offset, energy_local, OFFMAX)
        own_less, own_great = mixed_sums(extended, own_weights, *settings)
        partner_less, partner_great = mixed_sums(extended, partner_weights, *settings)
        arrived = lax.ppermute(jnp.stack([partner_less, partner_great]), "kz", near_pairs)
        less_parts.append((own_less + arrived[0]).astype(jnp.bfloat16))
        great_parts.append((own_great + arrived[1]).astype(jnp.bfloat16))
    return (jnp.stack(less_parts, axis=2), jnp.stack(great_parts, axis=2))


def solution(mesh):
    in_specs = (
        P("kz", "en", None, None, None, None),
        P("kz", "en", None, None, None, None),
        P(),
        P(),
        P(),
        P(),
        P(),
        P(),
        P(),
        P(),
        P(),
    )
    out_specs = (P("kz", "en", None, None, None, None), P("kz", "en", None, None, None, None))
    return jax.shard_map(
        on_device, mesh=mesh, in_specs=in_specs, out_specs=out_specs, check_vma=False
    )
```

```python
import jax
import jax.numpy as jnp
from jax import lax
from jax.sharding import PartitionSpec as P
from jax.experimental import pallas as pl

OFFMAX = 4


DAMPING = 0.3


def padded(block, sides, width):
    for axis, dim in sides:
        count = lax.axis_size(axis)
        forward = [(i, i + 1) for i in range(count - 1)]
        backward = [(target, source) for source, target in forward]
        low = lax.ppermute(
            lax.slice_in_dim(block, block.shape[dim] - width, None, axis=dim), axis, forward
        )
        high = lax.ppermute(lax.slice_in_dim(block, 0, width, axis=dim), axis, backward)
        block = jnp.concatenate([low, block, high], axis=dim)
    return block


def matmul_high(left_matrix, right_matrix):
    return jnp.matmul(left_matrix, right_matrix, precision=lax.Precision.HIGHEST)


def complex_product(left_pair, right_pair):
    orbitals = left_pair[0].shape[-1]
    rows = jnp.concatenate([left_pair[0], left_pair[1]], axis=-2)
    cols = jnp.concatenate([right_pair[0], right_pair[1]], axis=-1)
    full = matmul_high(rows, cols)
    real_part = full[..., :orbitals, :orbitals] - full[..., orbitals:, orbitals:]
    imag_part = full[..., :orbitals, orbitals:] + full[..., orbitals:, :orbitals]
    return (real_part, imag_part)


def real_left(matrix, pair_value):
    orbitals = pair_value[0].shape[-1]
    full = matmul_high(matrix, jnp.concatenate([pair_value[0], pair_value[1]], axis=-1))
    return (full[..., :orbitals], full[..., orbitals:])


def real_right(pair_value, matrix):
    orbitals = pair_value[0].shape[-2]
    full = matmul_high(jnp.concatenate([pair_value[0], pair_value[1]], axis=-2), matrix)
    return (full[..., :orbitals, :], full[..., orbitals:, :])


def adjoint(pair_value):
    return (jnp.swapaxes(pair_value[0], -1, -2), -jnp.swapaxes(pair_value[1], -1, -2))


def add_pair(left_pair, right_pair):
    return (left_pair[0] + right_pair[0], left_pair[1] + right_pair[1])


def sub_pair(left_pair, right_pair):
    return (left_pair[0] - right_pair[0], left_pair[1] - right_pair[1])


def sweep_kernel(normal_re_ref, normal_im_ref, out_re_ref, out_im_ref):
    batch, orbitals, _ = normal_re_ref.shape
    out_re_ref[...] = normal_re_ref[...]
    out_im_ref[...] = normal_im_ref[...]
    lane = lax.broadcasted_iota(jnp.int32, (1, orbitals), 1)
    row_index = lax.broadcasted_iota(jnp.int32, (orbitals, 1), 0)

    def step(pivot, carry):
        lane_hit = lane == pivot
        row_hit = row_index == pivot
        for item in range(batch):
            whole_re = out_re_ref[item]
            whole_im = out_im_ref[item]
            row_re = out_re_ref[item, pl.ds(pivot, 1), :]
            row_im = out_im_ref[item, pl.ds(pivot, 1), :]
            col_re = jnp.sum(jnp.where(lane_hit, whole_re, 0.0), axis=1, keepdims=True)
            col_im = jnp.sum(jnp.where(lane_hit, whole_im, 0.0), axis=1, keepdims=True)
            piv_re = jnp.sum(jnp.where(lane_hit, row_re, 0.0), axis=1, keepdims=True)
            piv_im = jnp.sum(jnp.where(lane_hit, row_im, 0.0), axis=1, keepdims=True)
            norm = piv_re * piv_re + piv_im * piv_im
            inv_re = piv_re / norm
            inv_im = -piv_im / norm
            scaled_re = jnp.where(lane_hit, inv_re, row_re * inv_re - row_im * inv_im)
            scaled_im = jnp.where(lane_hit, inv_im, row_re * inv_im + row_im * inv_re)
            col_re = jnp.where(row_hit, 0.0, col_re)
            col_im = jnp.where(row_hit, 0.0, col_im)
            base_re = jnp.where(lane_hit, 0.0, whole_re)
            base_im = jnp.where(lane_hit, 0.0, whole_im)
            out_re_ref[item] = base_re - (col_re * scaled_re - col_im * scaled_im)
            out_im_ref[item] = base_im - (col_re * scaled_im + col_im * scaled_re)
            out_re_ref[item, pl.ds(pivot, 1), :] = scaled_re
            out_im_ref[item, pl.ds(pivot, 1), :] = scaled_im
        return carry

    lax.fori_loop(0, orbitals, step, 0)


def hermitian_inverse(normal_pair, interpret=False):
    shape = normal_pair[0].shape
    orbitals = shape[-1]
    flat = [item.reshape(-1, orbitals, orbitals) for item in normal_pair]
    out_shape = jax.ShapeDtypeStruct(flat[0].shape, jnp.float32)
    inverse = pl.pallas_call(
        sweep_kernel,
        out_shape=(out_shape, out_shape),
        interpret=interpret,
    )(*flat)
    return (inverse[0].reshape(shape), inverse[1].reshape(shape))


def invert_pair(pair_value, interpret=False):
    adjoint_value = adjoint(pair_value)
    normal = complex_product(adjoint_value, pair_value)
    normal_inverse = hermitian_inverse(normal, interpret)
    return complex_product(normal_inverse, adjoint_value)


def greater_of(less_pair, ret_pair):
    return sub_pair(add_pair(less_pair, ret_pair), adjoint(ret_pair))


def pack_pair(pair_value):
    return jnp.stack([pair_value[0], pair_value[1]], axis=-3)


def green_blocks(sigma_less, sigma_great, hamilton, slab_coupling, energies):
    orbitals = sigma_less.shape[-1]
    slab_count = sigma_less.shape[2]
    identity = jnp.eye(orbitals, dtype=jnp.float32)
    energy_grid = energies[None, :, None, None]
    left_ret = []
    left_less = []
    for slab_index in range(slab_count):
        lesser = sigma_less[:, :, slab_index].astype(jnp.float32)
        greater = sigma_great[:, :, slab_index].astype(jnp.float32)
        retarded_re = 0.5 * (greater[:, :, 0] - lesser[:, :, 0])
        retarded_im = 0.5 * (greater[:, :, 1] - lesser[:, :, 1]) - DAMPING * identity
        system_re = energy_grid * identity - hamilton[:, :, slab_index] - retarded_re
        system_im = -retarded_im
        source = (lesser[:, :, 0], lesser[:, :, 1])
        if slab_index > 0:
            coupling = slab_coupling[slab_index - 1]
            folded = real_right(real_left(coupling, left_ret[-1]), coupling.T)
            system_re = system_re - folded[0]
            system_im = system_im - folded[1]
            source = add_pair(source, real_right(real_left(coupling, left_less[-1]), coupling.T))
        inverse = invert_pair((system_re, system_im))
        left_ret.append(inverse)
        left_less.append(complex_product(complex_product(inverse, source), adjoint(inverse)))
    full_ret = left_ret[-1]
    full_less = left_less[-1]
    lesser_list = [full_less]
    greater_list = [greater_of(full_less, full_ret)]
    for slab_index in range(slab_count - 2, -1, -1):
        coupling = slab_coupling[slab_index]
        green_couple = real_right(left_ret[slab_index], coupling)
        bridge = real_right(complex_product(green_couple, full_ret), coupling.T)
        cross_term = complex_product(bridge, left_less[slab_index])
        spread = complex_product(
            real_right(complex_product(green_couple, full_less), coupling.T),
            adjoint(left_ret[slab_index]),
        )
        full_less = add_pair(
            add_pair(left_less[slab_index], spread), sub_pair(cross_term, adjoint(cross_term))
        )
        full_ret = add_pair(left_ret[slab_index], complex_product(bridge, left_ret[slab_index]))
        lesser_list.insert(0, full_less)
        greater_list.insert(0, greater_of(full_less, full_ret))
    return [
        jnp.stack([pack_pair(less_item), pack_pair(great_item)], axis=2).astype(jnp.bfloat16)
        for less_item, great_item in zip(lesser_list, greater_list)
    ]


def hamiltonian(onsite_table, cos_coupling, slab_kind, momenta_index, momenta_total):
    kind_count = onsite_table.shape[0]
    choose = (slab_kind[:, None] == jnp.arange(kind_count, dtype=jnp.int32)[None, :]).astype(
        jnp.float32
    )
    onsite = jnp.einsum("sk,kij->sij", choose, onsite_table, precision=lax.Precision.HIGHEST)
    phase_factor = jnp.cos(2.0 * jnp.pi * momenta_index.astype(jnp.float32) / momenta_total)
    hamilton = onsite[None] + phase_factor[:, None, None, None] * cos_coupling[None]
    return hamilton[:, None]


def momentum_weights(table_rows, mode_weight, momenta_total):
    onehot = (
        table_rows[:, :, None] == jnp.arange(momenta_total, dtype=jnp.int32)[None, None, :]
    ).astype(jnp.float32)
    return (
        jnp.einsum("lq,aqk->lak", mode_weight, onehot, precision=lax.Precision.HIGHEST)
        / momenta_total
    )


def mixed_sums(extended, weights, form_factor, occupation, energy_offset, energy_count, margin):
    total_less = None
    total_great = None
    for mode_index in range(form_factor.shape[0]):
        shift_steps = energy_offset[mode_index]
        upper_side = lax.dynamic_slice_in_dim(extended, margin + shift_steps, energy_count, 1)
        lower_side = lax.dynamic_slice_in_dim(extended, margin - shift_steps, energy_count, 1)
        occupied = occupation[mode_index]
        less_term = (occupied + 1.0) * upper_side[:, :, 0].astype(
            jnp.float32
        ) + occupied * lower_side[:, :, 0].astype(jnp.float32)
        great_term = (occupied + 1.0) * lower_side[:, :, 1].astype(
            jnp.float32
        ) + occupied * upper_side[:, :, 1].astype(jnp.float32)
        mode_weights = weights[mode_index].reshape(
            weights.shape[1:] + (1,) * (less_term.ndim - 1)
        )
        less_sum = form_factor[mode_index] * jnp.sum(mode_weights * less_term[None], axis=1)
        great_sum = form_factor[mode_index] * jnp.sum(mode_weights * great_term[None], axis=1)
        total_less = less_sum if total_less is None else total_less + less_sum
        total_great = great_sum if total_great is None else total_great + great_sum
    return (total_less, total_great)


def exchange_blocks(blocks, width):
    count = lax.axis_size("kz")
    lanes = lax.axis_size("en")

    def far_of(index):
        return (index + 2) % count

    def joint(index, lane):
        return index * lanes + lane

    far = lax.ppermute(blocks, "kz", [(i, far_of(i)) for i in range(count)])
    tail = lax.slice_in_dim(blocks, blocks.shape[1] - width, None, axis=1)
    head = lax.slice_in_dim(blocks, 0, width, axis=1)
    forward = [(lane, lane + 1) for lane in range(lanes - 1)]
    backward = [(lane + 1, lane) for lane in range(lanes - 1)]
    low_same = lax.ppermute(tail, "en", forward)
    high_same = lax.ppermute(head, "en", backward)
    low_far = lax.ppermute(
        tail,
        ("kz", "en"),
        [(joint(far_of(i), lane), joint(i, lane + 1)) for i in range(count) for lane in range(lanes - 1)],
    )
    high_far = lax.ppermute(
        head,
        ("kz", "en"),
        [(joint(far_of(i), lane + 1), joint(i, lane)) for i in range(count) for lane in range(lanes - 1)],
    )
    own_extended = jnp.concatenate([low_same, blocks, high_same], axis=1)
    far_extended = jnp.concatenate([low_far, far, high_far], axis=1)
    return jnp.concatenate([own_extended, far_extended], axis=0)


def on_device(
    sigma_less,
    sigma_great,
    onsite_table,
    cos_coupling,
    slab_coupling,
    slab_kind,
    kz_table,
    mode_weight,
    form_factor,
    occupation,
    energy_offset,
):
    momenta_local = sigma_less.shape[0]
    energy_local = sigma_less.shape[1]
    momenta_total = momenta_local * lax.axis_size("kz")
    energy_total = energy_local * lax.axis_size("en")
    momenta_start = lax.axis_index("kz") * momenta_local
    momenta_index = momenta_start + jnp.arange(momenta_local, dtype=jnp.int32)
    energy_index = lax.axis_index("en") * energy_local + jnp.arange(energy_local, dtype=jnp.int32)
    energies = -1.5 + 3.0 * (energy_index.astype(jnp.float32) + 0.5) / energy_total
    hamilton = hamiltonian(onsite_table, cos_coupling, slab_kind, momenta_index, momenta_total)
    slab_blocks = green_blocks(sigma_less, sigma_great, hamilton, slab_coupling, energies)
    count = lax.axis_size("kz")
    momentum = lax.axis_index("kz")
    partner = momentum ^ 1
    held = jnp.stack([momentum, (momentum + 2) % count])
    all_weights = momentum_weights(kz_table, mode_weight, momenta_total)
    own_weights = jnp.take(jnp.take(all_weights, momentum[None], axis=1), held, axis=2)
    partner_weights = jnp.take(jnp.take(all_weights, partner[None], axis=1), held, axis=2)
    near_pairs = [(i, i ^ 1) for i in range(count)]
    less_parts = []
    great_parts = []
    for blocks in slab_blocks:
        extended = exchange_blocks(blocks, OFFMAX)
        settings = (form_factor, occupation, energy_offset, energy_local, OFFMAX)
        own_less, own_great = mixed_sums(extended, own_weights, *settings)
        partner_less, partner_great = mixed_sums(extended, partner_weights, *settings)
        arrived = lax.ppermute(jnp.stack([partner_less, partner_great]), "kz", near_pairs)
        less_parts.append((own_less + arrived[0]).astype(jnp.bfloat16))
        great_parts.append((own_great + arrived[1]).astype(jnp.bfloat16))
    return (jnp.stack(less_parts, axis=2), jnp.stack(great_parts, axis=2))


def solution(mesh):
    in_specs = (
        P("kz", "en", None, None, None, None),
        P("kz", "en", None, None, None, None),
        P(),
        P(),
        P(),
        P(),
        P(),
        P(),
        P(),
        P(),
        P(),
    )
    out_specs = (P("kz", "en", None, None, None, None), P("kz", "en", None, None, None, None))
    return jax.shard_map(
        on_device, mesh=mesh, in_specs=in_specs, out_specs=out_specs, check_vma=False
    )
```

```python
import jax
import jax.numpy as jnp
from jax import lax
from jax.sharding import PartitionSpec as P
from jax.experimental import pallas as pl

OFFMAX = 4


DAMPING = 0.3


def padded(block, sides, width):
    for axis, dim in sides:
        count = lax.axis_size(axis)
        forward = [(i, i + 1) for i in range(count - 1)]
        backward = [(target, source) for source, target in forward]
        low = lax.ppermute(
            lax.slice_in_dim(block, block.shape[dim] - width, None, axis=dim), axis, forward
        )
        high = lax.ppermute(lax.slice_in_dim(block, 0, width, axis=dim), axis, backward)
        block = jnp.concatenate([low, block, high], axis=dim)
    return block


def matmul_high(left_matrix, right_matrix):
    return jnp.matmul(left_matrix, right_matrix, precision=lax.Precision.HIGHEST)


def complex_product(left_pair, right_pair):
    orbitals = left_pair[0].shape[-1]
    rows = jnp.concatenate([left_pair[0], left_pair[1]], axis=-2)
    cols = jnp.concatenate([right_pair[0], right_pair[1]], axis=-1)
    full = matmul_high(rows, cols)
    real_part = full[..., :orbitals, :orbitals] - full[..., orbitals:, orbitals:]
    imag_part = full[..., :orbitals, orbitals:] + full[..., orbitals:, :orbitals]
    return (real_part, imag_part)


def real_left(matrix, pair_value):
    orbitals = pair_value[0].shape[-1]
    full = matmul_high(matrix, jnp.concatenate([pair_value[0], pair_value[1]], axis=-1))
    return (full[..., :orbitals], full[..., orbitals:])


def real_right(pair_value, matrix):
    orbitals = pair_value[0].shape[-2]
    full = matmul_high(jnp.concatenate([pair_value[0], pair_value[1]], axis=-2), matrix)
    return (full[..., :orbitals, :], full[..., orbitals:, :])


def adjoint(pair_value):
    return (jnp.swapaxes(pair_value[0], -1, -2), -jnp.swapaxes(pair_value[1], -1, -2))


def add_pair(left_pair, right_pair):
    return (left_pair[0] + right_pair[0], left_pair[1] + right_pair[1])


def sub_pair(left_pair, right_pair):
    return (left_pair[0] - right_pair[0], left_pair[1] - right_pair[1])


def sweep_kernel(normal_re_ref, normal_im_ref, out_re_ref, out_im_ref):
    batch, orbitals, _ = normal_re_ref.shape
    out_re_ref[...] = normal_re_ref[...]
    out_im_ref[...] = normal_im_ref[...]
    lane = lax.broadcasted_iota(jnp.int32, (1, orbitals), 1)
    row_index = lax.broadcasted_iota(jnp.int32, (orbitals, 1), 0)

    def step(pivot, carry):
        lane_hit = lane == pivot
        row_hit = row_index == pivot
        for item in range(batch):
            whole_re = out_re_ref[item]
            whole_im = out_im_ref[item]
            row_re = out_re_ref[item, pl.ds(pivot, 1), :]
            row_im = out_im_ref[item, pl.ds(pivot, 1), :]
            col_re = jnp.sum(jnp.where(lane_hit, whole_re, 0.0), axis=1, keepdims=True)
            col_im = jnp.sum(jnp.where(lane_hit, whole_im, 0.0), axis=1, keepdims=True)
            piv_re = jnp.sum(jnp.where(lane_hit, row_re, 0.0), axis=1, keepdims=True)
            piv_im = jnp.sum(jnp.where(lane_hit, row_im, 0.0), axis=1, keepdims=True)
            norm = piv_re * piv_re + piv_im * piv_im
            inv_re = piv_re / norm
            inv_im = -piv_im / norm
            scaled_re = jnp.where(lane_hit, inv_re, row_re * inv_re - row_im * inv_im)
            scaled_im = jnp.where(lane_hit, inv_im, row_re * inv_im + row_im * inv_re)
            col_re = jnp.where(row_hit, 0.0, col_re)
            col_im = jnp.where(row_hit, 0.0, col_im)
            base_re = jnp.where(lane_hit, 0.0, whole_re)
            base_im = jnp.where(lane_hit, 0.0, whole_im)
            out_re_ref[item] = base_re - (col_re * scaled_re - col_im * scaled_im)
            out_im_ref[item] = base_im - (col_re * scaled_im + col_im * scaled_re)
            out_re_ref[item, pl.ds(pivot, 1), :] = scaled_re
            out_im_ref[item, pl.ds(pivot, 1), :] = scaled_im
        return carry

    lax.fori_loop(0, orbitals, step, 0)


def hermitian_inverse(normal_pair, interpret=False):
    shape = normal_pair[0].shape
    orbitals = shape[-1]
    flat = [item.reshape(-1, orbitals, orbitals) for item in normal_pair]
    out_shape = jax.ShapeDtypeStruct(flat[0].shape, jnp.float32)
    inverse = pl.pallas_call(
        sweep_kernel,
        out_shape=(out_shape, out_shape),
        interpret=interpret,
    )(*flat)
    return (inverse[0].reshape(shape), inverse[1].reshape(shape))


def invert_pair(pair_value, interpret=False):
    adjoint_value = adjoint(pair_value)
    normal = complex_product(adjoint_value, pair_value)
    normal_inverse = hermitian_inverse(normal, interpret)
    return complex_product(normal_inverse, adjoint_value)


def greater_of(less_pair, ret_pair):
    return sub_pair(add_pair(less_pair, ret_pair), adjoint(ret_pair))


def pack_pair(pair_value):
    return jnp.stack([pair_value[0], pair_value[1]], axis=-3)


def green_blocks(sigma_less, sigma_great, hamilton, slab_coupling, energies):
    orbitals = sigma_less.shape[-1]
    slab_count = sigma_less.shape[2]
    identity = jnp.eye(orbitals, dtype=jnp.float32)
    energy_grid = energies[None, :, None, None]
    left_ret = []
    left_less = []
    for slab_index in range(slab_count):
        lesser = sigma_less[:, :, slab_index].astype(jnp.float32)
        greater = sigma_great[:, :, slab_index].astype(jnp.float32)
        retarded_re = 0.5 * (greater[:, :, 0] - lesser[:, :, 0])
        retarded_im = 0.5 * (greater[:, :, 1] - lesser[:, :, 1]) - DAMPING * identity
        system_re = energy_grid * identity - hamilton[:, :, slab_index] - retarded_re
        system_im = -retarded_im
        source = (lesser[:, :, 0], lesser[:, :, 1])
        if slab_index > 0:
            coupling = slab_coupling[slab_index - 1]
            folded = real_right(real_left(coupling, left_ret[-1]), coupling.T)
            system_re = system_re - folded[0]
            system_im = system_im - folded[1]
            source = add_pair(source, real_right(real_left(coupling, left_less[-1]), coupling.T))
        inverse = invert_pair((system_re, system_im))
        left_ret.append(inverse)
        left_less.append(complex_product(complex_product(inverse, source), adjoint(inverse)))
    full_ret = left_ret[-1]
    full_less = left_less[-1]
    lesser_list = [full_less]
    greater_list = [greater_of(full_less, full_ret)]
    for slab_index in range(slab_count - 2, -1, -1):
        coupling = slab_coupling[slab_index]
        green_couple = real_right(left_ret[slab_index], coupling)
        bridge = real_right(complex_product(green_couple, full_ret), coupling.T)
        cross_term = complex_product(bridge, left_less[slab_index])
        spread = complex_product(
            real_right(complex_product(green_couple, full_less), coupling.T),
            adjoint(left_ret[slab_index]),
        )
        full_less = add_pair(
            add_pair(left_less[slab_index], spread), sub_pair(cross_term, adjoint(cross_term))
        )
        full_ret = add_pair(left_ret[slab_index], complex_product(bridge, left_ret[slab_index]))
        lesser_list.insert(0, full_less)
        greater_list.insert(0, greater_of(full_less, full_ret))
    return [
        jnp.stack([pack_pair(less_item), pack_pair(great_item)], axis=2).astype(jnp.bfloat16)
        for less_item, great_item in zip(lesser_list, greater_list)
    ]


def hamiltonian(onsite_table, cos_coupling, slab_kind, momenta_index, momenta_total):
    kind_count = onsite_table.shape[0]
    choose = (slab_kind[:, None] == jnp.arange(kind_count, dtype=jnp.int32)[None, :]).astype(
        jnp.float32
    )
    onsite = jnp.einsum("sk,kij->sij", choose, onsite_table, precision=lax.Precision.HIGHEST)
    phase_factor = jnp.cos(2.0 * jnp.pi * momenta_index.astype(jnp.float32) / momenta_total)
    hamilton = onsite[None] + phase_factor[:, None, None, None] * cos_coupling[None]
    return hamilton[:, None]


def momentum_weights(table_rows, mode_weight, momenta_total):
    onehot = (
        table_rows[:, :, None] == jnp.arange(momenta_total, dtype=jnp.int32)[None, None, :]
    ).astype(jnp.float32)
    return (
        jnp.einsum("lq,aqk->lak", mode_weight, onehot, precision=lax.Precision.HIGHEST)
        / momenta_total
    )


def mixed_sums(extended, weights, form_factor, occupation, energy_offset, energy_count, margin):
    total_less = None
    total_great = None
    for mode_index in range(form_factor.shape[0]):
        shift_steps = energy_offset[mode_index]
        upper_side = lax.dynamic_slice_in_dim(extended, margin + shift_steps, energy_count, 1)
        lower_side = lax.dynamic_slice_in_dim(extended, margin - shift_steps, energy_count, 1)
        occupied = occupation[mode_index]
        less_term = (occupied + 1.0) * upper_side[:, :, 0].astype(
            jnp.float32
        ) + occupied * lower_side[:, :, 0].astype(jnp.float32)
        great_term = (occupied + 1.0) * lower_side[:, :, 1].astype(
            jnp.float32
        ) + occupied * upper_side[:, :, 1].astype(jnp.float32)
        mode_weights = weights[mode_index].reshape(
            weights.shape[1:] + (1,) * (less_term.ndim - 1)
        )
        less_sum = form_factor[mode_index] * jnp.sum(mode_weights * less_term[None], axis=1)
        great_sum = form_factor[mode_index] * jnp.sum(mode_weights * great_term[None], axis=1)
        total_less = less_sum if total_less is None else total_less + less_sum
        total_great = great_sum if total_great is None else total_great + great_sum
    return (total_less, total_great)


def exchange_blocks(blocks, width):
    count = lax.axis_size("kz")
    lanes = lax.axis_size("en")

    def far_of(index):
        return (index + 2) % count

    def joint(index, lane):
        return index * lanes + lane

    far = lax.ppermute(blocks, "kz", [(i, far_of(i)) for i in range(count)])
    tail = lax.slice_in_dim(blocks, blocks.shape[1] - width, None, axis=1)
    head = lax.slice_in_dim(blocks, 0, width, axis=1)
    forward = [(lane, lane + 1) for lane in range(lanes - 1)]
    backward = [(lane + 1, lane) for lane in range(lanes - 1)]
    low_same = lax.ppermute(tail, "en", forward)
    high_same = lax.ppermute(head, "en", backward)
    low_far = lax.ppermute(
        tail,
        ("kz", "en"),
        [(joint(far_of(i), lane), joint(i, lane + 1)) for i in range(count) for lane in range(lanes - 1)],
    )
    high_far = lax.ppermute(
        head,
        ("kz", "en"),
        [(joint(far_of(i), lane + 1), joint(i, lane)) for i in range(count) for lane in range(lanes - 1)],
    )
    own_extended = jnp.concatenate([low_same, blocks, high_same], axis=1)
    far_extended = jnp.concatenate([low_far, far, high_far], axis=1)
    return jnp.concatenate([own_extended, far_extended], axis=0)


def on_device(
    sigma_less,
    sigma_great,
    onsite_table,
    cos_coupling,
    slab_coupling,
    slab_kind,
    kz_table,
    mode_weight,
    form_factor,
    occupation,
    energy_offset,
):
    momenta_local = sigma_less.shape[0]
    energy_local = sigma_less.shape[1]
    momenta_total = momenta_local * lax.axis_size("kz")
    energy_total = energy_local * lax.axis_size("en")
    momenta_start = lax.axis_index("kz") * momenta_local
    momenta_index = momenta_start + jnp.arange(momenta_local, dtype=jnp.int32)
    energy_index = lax.axis_index("en") * energy_local + jnp.arange(energy_local, dtype=jnp.int32)
    energies = -1.5 + 3.0 * (energy_index.astype(jnp.float32) + 0.5) / energy_total
    hamilton = hamiltonian(onsite_table, cos_coupling, slab_kind, momenta_index, momenta_total)
    slab_blocks = green_blocks(sigma_less, sigma_great, hamilton, slab_coupling, energies)
    count = lax.axis_size("kz")
    momentum = lax.axis_index("kz")
    partner = momentum ^ 1
    held = jnp.stack([momentum, (momentum + 2) % count])
    all_weights = momentum_weights(kz_table, mode_weight, momenta_total)
    own_weights = jnp.take(jnp.take(all_weights, momentum[None], axis=1), held, axis=2)
    partner_weights = jnp.take(jnp.take(all_weights, partner[None], axis=1), held, axis=2)
    near_pairs = [(i, i ^ 1) for i in range(count)]
    less_parts = []
    great_parts = []
    slab_total = len(slab_blocks)
    groups = [list(range(slab_total - 1)), [slab_total - 1]] if slab_total > 1 else [[0]]
    for group in groups:
        blocks = jnp.stack([slab_blocks[slab_index] for slab_index in group], axis=3)
        extended = exchange_blocks(blocks, OFFMAX)
        settings = (form_factor, occupation, energy_offset, energy_local, OFFMAX)
        own_less, own_great = mixed_sums(extended, own_weights, *settings)
        partner_less, partner_great = mixed_sums(extended, partner_weights, *settings)
        arrived = lax.ppermute(jnp.stack([partner_less, partner_great]), "kz", near_pairs)
        less_parts.append((own_less + arrived[0]).astype(jnp.bfloat16))
        great_parts.append((own_great + arrived[1]).astype(jnp.bfloat16))
    return (jnp.concatenate(less_parts, axis=2), jnp.concatenate(great_parts, axis=2))


def solution(mesh):
    in_specs = (
        P("kz", "en", None, None, None, None),
        P("kz", "en", None, None, None, None),
        P(),
        P(),
        P(),
        P(),
        P(),
        P(),
        P(),
        P(),
        P(),
    )
    out_specs = (P("kz", "en", None, None, None, None), P("kz", "en", None, None, None, None))
    return jax.shard_map(
        on_device, mesh=mesh, in_specs=in_specs, out_specs=out_specs, check_vma=False
    )
```

```python
import jax
import jax.numpy as jnp
from jax import lax
from jax.sharding import PartitionSpec as P
from jax.experimental import pallas as pl

OFFMAX = 4


DAMPING = 0.3


def padded(block, sides, width):
    for axis, dim in sides:
        count = lax.axis_size(axis)
        forward = [(i, i + 1) for i in range(count - 1)]
        backward = [(target, source) for source, target in forward]
        low = lax.ppermute(
            lax.slice_in_dim(block, block.shape[dim] - width, None, axis=dim), axis, forward
        )
        high = lax.ppermute(lax.slice_in_dim(block, 0, width, axis=dim), axis, backward)
        block = jnp.concatenate([low, block, high], axis=dim)
    return block


def matmul_high(left_matrix, right_matrix):
    return jnp.matmul(left_matrix, right_matrix, precision=lax.Precision.HIGHEST)


def complex_product(left_pair, right_pair):
    orbitals = left_pair[0].shape[-1]
    rows = jnp.concatenate([left_pair[0], left_pair[1]], axis=-2)
    cols = jnp.concatenate([right_pair[0], right_pair[1]], axis=-1)
    full = matmul_high(rows, cols)
    real_part = full[..., :orbitals, :orbitals] - full[..., orbitals:, orbitals:]
    imag_part = full[..., :orbitals, orbitals:] + full[..., orbitals:, :orbitals]
    return (real_part, imag_part)


def real_left(matrix, pair_value):
    orbitals = pair_value[0].shape[-1]
    full = matmul_high(matrix, jnp.concatenate([pair_value[0], pair_value[1]], axis=-1))
    return (full[..., :orbitals], full[..., orbitals:])


def real_right(pair_value, matrix):
    orbitals = pair_value[0].shape[-2]
    full = matmul_high(jnp.concatenate([pair_value[0], pair_value[1]], axis=-2), matrix)
    return (full[..., :orbitals, :], full[..., orbitals:, :])


def adjoint(pair_value):
    return (jnp.swapaxes(pair_value[0], -1, -2), -jnp.swapaxes(pair_value[1], -1, -2))


def add_pair(left_pair, right_pair):
    return (left_pair[0] + right_pair[0], left_pair[1] + right_pair[1])


def sub_pair(left_pair, right_pair):
    return (left_pair[0] - right_pair[0], left_pair[1] - right_pair[1])


def sweep_kernel(normal_re_ref, normal_im_ref, out_re_ref, out_im_ref):
    batch, orbitals, _ = normal_re_ref.shape
    out_re_ref[...] = normal_re_ref[...]
    out_im_ref[...] = normal_im_ref[...]
    lane = lax.broadcasted_iota(jnp.int32, (1, orbitals), 1)
    row_index = lax.broadcasted_iota(jnp.int32, (orbitals, 1), 0)

    def step(pivot, carry):
        lane_hit = lane == pivot
        row_hit = row_index == pivot
        for item in range(batch):
            whole_re = out_re_ref[item]
            whole_im = out_im_ref[item]
            row_re = out_re_ref[item, pl.ds(pivot, 1), :]
            row_im = out_im_ref[item, pl.ds(pivot, 1), :]
            col_re = jnp.sum(jnp.where(lane_hit, whole_re, 0.0), axis=1, keepdims=True)
            col_im = jnp.sum(jnp.where(lane_hit, whole_im, 0.0), axis=1, keepdims=True)
            piv_re = jnp.sum(jnp.where(lane_hit, row_re, 0.0), axis=1, keepdims=True)
            piv_im = jnp.sum(jnp.where(lane_hit, row_im, 0.0), axis=1, keepdims=True)
            norm = piv_re * piv_re + piv_im * piv_im
            inv_re = piv_re / norm
            inv_im = -piv_im / norm
            product_re = row_re * inv_re - row_im * inv_im
            product_im = row_re * inv_im + row_im * inv_re
            scaled_re = jnp.where(lane_hit, inv_re, product_re)
            scaled_im = jnp.where(lane_hit, inv_im, product_im)
            update_re = jnp.where(lane_hit, inv_re + 1.0, product_re)
            update_im = scaled_im
            col_re = jnp.where(row_hit, 0.0, col_re)
            col_im = jnp.where(row_hit, 0.0, col_im)
            out_re_ref[item] = whole_re - (col_re * update_re - col_im * update_im)
            out_im_ref[item] = whole_im - (col_re * update_im + col_im * update_re)
            out_re_ref[item, pl.ds(pivot, 1), :] = scaled_re
            out_im_ref[item, pl.ds(pivot, 1), :] = scaled_im
        return carry

    lax.fori_loop(0, orbitals, step, 0)


def hermitian_inverse(normal_pair, interpret=False):
    shape = normal_pair[0].shape
    orbitals = shape[-1]
    flat = [item.reshape(-1, orbitals, orbitals) for item in normal_pair]
    out_shape = jax.ShapeDtypeStruct(flat[0].shape, jnp.float32)
    inverse = pl.pallas_call(
        sweep_kernel,
        out_shape=(out_shape, out_shape),
        interpret=interpret,
    )(*flat)
    return (inverse[0].reshape(shape), inverse[1].reshape(shape))


def invert_pair(pair_value, interpret=False):
    adjoint_value = adjoint(pair_value)
    normal = complex_product(adjoint_value, pair_value)
    normal_inverse = hermitian_inverse(normal, interpret)
    return complex_product(normal_inverse, adjoint_value)


def greater_of(less_pair, ret_pair):
    return sub_pair(add_pair(less_pair, ret_pair), adjoint(ret_pair))


def pack_pair(pair_value):
    return jnp.stack([pair_value[0], pair_value[1]], axis=-3)


def green_blocks(sigma_less, sigma_great, hamilton, slab_coupling, energies):
    orbitals = sigma_less.shape[-1]
    slab_count = sigma_less.shape[2]
    identity = jnp.eye(orbitals, dtype=jnp.float32)
    energy_grid = energies[None, :, None, None]
    left_ret = []
    left_less = []
    for slab_index in range(slab_count):
        lesser = sigma_less[:, :, slab_index].astype(jnp.float32)
        greater = sigma_great[:, :, slab_index].astype(jnp.float32)
        retarded_re = 0.5 * (greater[:, :, 0] - lesser[:, :, 0])
        retarded_im = 0.5 * (greater[:, :, 1] - lesser[:, :, 1]) - DAMPING * identity
        system_re = energy_grid * identity - hamilton[:, :, slab_index] - retarded_re
        system_im = -retarded_im
        source = (lesser[:, :, 0], lesser[:, :, 1])
        if slab_index > 0:
            coupling = slab_coupling[slab_index - 1]
            folded = real_right(real_left(coupling, left_ret[-1]), coupling.T)
            system_re = system_re - folded[0]
            system_im = system_im - folded[1]
            source = add_pair(source, real_right(real_left(coupling, left_less[-1]), coupling.T))
        inverse = invert_pair((system_re, system_im))
        left_ret.append(inverse)
        left_less.append(complex_product(complex_product(inverse, source), adjoint(inverse)))
    full_ret = left_ret[-1]
    full_less = left_less[-1]
    lesser_list = [full_less]
    greater_list = [greater_of(full_less, full_ret)]
    for slab_index in range(slab_count - 2, -1, -1):
        coupling = slab_coupling[slab_index]
        green_couple = real_right(left_ret[slab_index], coupling)
        bridge = real_right(complex_product(green_couple, full_ret), coupling.T)
        cross_term = complex_product(bridge, left_less[slab_index])
        spread = complex_product(
            real_right(complex_product(green_couple, full_less), coupling.T),
            adjoint(left_ret[slab_index]),
        )
        full_less = add_pair(
            add_pair(left_less[slab_index], spread), sub_pair(cross_term, adjoint(cross_term))
        )
        full_ret = add_pair(left_ret[slab_index], complex_product(bridge, left_ret[slab_index]))
        lesser_list.insert(0, full_less)
        greater_list.insert(0, greater_of(full_less, full_ret))
    return [
        jnp.stack([pack_pair(less_item), pack_pair(great_item)], axis=2).astype(jnp.bfloat16)
        for less_item, great_item in zip(lesser_list, greater_list)
    ]


def hamiltonian(onsite_table, cos_coupling, slab_kind, momenta_index, momenta_total):
    kind_count = onsite_table.shape[0]
    choose = (slab_kind[:, None] == jnp.arange(kind_count, dtype=jnp.int32)[None, :]).astype(
        jnp.float32
    )
    onsite = jnp.einsum("sk,kij->sij", choose, onsite_table, precision=lax.Precision.HIGHEST)
    phase_factor = jnp.cos(2.0 * jnp.pi * momenta_index.astype(jnp.float32) / momenta_total)
    hamilton = onsite[None] + phase_factor[:, None, None, None] * cos_coupling[None]
    return hamilton[:, None]


def momentum_weights(table_rows, mode_weight, momenta_total):
    onehot = (
        table_rows[:, :, None] == jnp.arange(momenta_total, dtype=jnp.int32)[None, None, :]
    ).astype(jnp.float32)
    return (
        jnp.einsum("lq,aqk->lak", mode_weight, onehot, precision=lax.Precision.HIGHEST)
        / momenta_total
    )


def mixed_sums(extended, weights, form_factor, occupation, energy_offset, energy_count, margin):
    total_less = None
    total_great = None
    for mode_index in range(form_factor.shape[0]):
        shift_steps = energy_offset[mode_index]
        upper_side = lax.dynamic_slice_in_dim(extended, margin + shift_steps, energy_count, 1)
        lower_side = lax.dynamic_slice_in_dim(extended, margin - shift_steps, energy_count, 1)
        occupied = occupation[mode_index]
        less_term = (occupied + 1.0) * upper_side[:, :, 0].astype(
            jnp.float32
        ) + occupied * lower_side[:, :, 0].astype(jnp.float32)
        great_term = (occupied + 1.0) * lower_side[:, :, 1].astype(
            jnp.float32
        ) + occupied * upper_side[:, :, 1].astype(jnp.float32)
        mode_weights = weights[mode_index].reshape(
            weights.shape[1:] + (1,) * (less_term.ndim - 1)
        )
        less_sum = form_factor[mode_index] * jnp.sum(mode_weights * less_term[None], axis=1)
        great_sum = form_factor[mode_index] * jnp.sum(mode_weights * great_term[None], axis=1)
        total_less = less_sum if total_less is None else total_less + less_sum
        total_great = great_sum if total_great is None else total_great + great_sum
    return (total_less, total_great)


def exchange_blocks(blocks, width):
    count = lax.axis_size("kz")
    lanes = lax.axis_size("en")

    def far_of(index):
        return (index + 2) % count

    def joint(index, lane):
        return index * lanes + lane

    far = lax.ppermute(blocks, "kz", [(i, far_of(i)) for i in range(count)])
    tail = lax.slice_in_dim(blocks, blocks.shape[1] - width, None, axis=1)
    head = lax.slice_in_dim(blocks, 0, width, axis=1)
    forward = [(lane, lane + 1) for lane in range(lanes - 1)]
    backward = [(lane + 1, lane) for lane in range(lanes - 1)]
    low_same = lax.ppermute(tail, "en", forward)
    high_same = lax.ppermute(head, "en", backward)
    low_far = lax.ppermute(
        tail,
        ("kz", "en"),
        [(joint(far_of(i), lane), joint(i, lane + 1)) for i in range(count) for lane in range(lanes - 1)],
    )
    high_far = lax.ppermute(
        head,
        ("kz", "en"),
        [(joint(far_of(i), lane + 1), joint(i, lane)) for i in range(count) for lane in range(lanes - 1)],
    )
    own_extended = jnp.concatenate([low_same, blocks, high_same], axis=1)
    far_extended = jnp.concatenate([low_far, far, high_far], axis=1)
    return jnp.concatenate([own_extended, far_extended], axis=0)


def on_device(
    sigma_less,
    sigma_great,
    onsite_table,
    cos_coupling,
    slab_coupling,
    slab_kind,
    kz_table,
    mode_weight,
    form_factor,
    occupation,
    energy_offset,
):
    momenta_local = sigma_less.shape[0]
    energy_local = sigma_less.shape[1]
    momenta_total = momenta_local * lax.axis_size("kz")
    energy_total = energy_local * lax.axis_size("en")
    momenta_start = lax.axis_index("kz") * momenta_local
    momenta_index = momenta_start + jnp.arange(momenta_local, dtype=jnp.int32)
    energy_index = lax.axis_index("en") * energy_local + jnp.arange(energy_local, dtype=jnp.int32)
    energies = -1.5 + 3.0 * (energy_index.astype(jnp.float32) + 0.5) / energy_total
    hamilton = hamiltonian(onsite_table, cos_coupling, slab_kind, momenta_index, momenta_total)
    slab_blocks = green_blocks(sigma_less, sigma_great, hamilton, slab_coupling, energies)
    count = lax.axis_size("kz")
    momentum = lax.axis_index("kz")
    partner = momentum ^ 1
    held = jnp.stack([momentum, (momentum + 2) % count])
    all_weights = momentum_weights(kz_table, mode_weight, momenta_total)
    own_weights = jnp.take(jnp.take(all_weights, momentum[None], axis=1), held, axis=2)
    partner_weights = jnp.take(jnp.take(all_weights, partner[None], axis=1), held, axis=2)
    near_pairs = [(i, i ^ 1) for i in range(count)]
    less_parts = []
    great_parts = []
    for blocks in slab_blocks:
        extended = exchange_blocks(blocks, OFFMAX)
        settings = (form_factor, occupation, energy_offset, energy_local, OFFMAX)
        own_less, own_great = mixed_sums(extended, own_weights, *settings)
        partner_less, partner_great = mixed_sums(extended, partner_weights, *settings)
        arrived = lax.ppermute(jnp.stack([partner_less, partner_great]), "kz", near_pairs)
        less_parts.append((own_less + arrived[0]).astype(jnp.bfloat16))
        great_parts.append((own_great + arrived[1]).astype(jnp.bfloat16))
    return (jnp.stack(less_parts, axis=2), jnp.stack(great_parts, axis=2))


def solution(mesh):
    in_specs = (
        P("kz", "en", None, None, None, None),
        P("kz", "en", None, None, None, None),
        P(),
        P(),
        P(),
        P(),
        P(),
        P(),
        P(),
        P(),
        P(),
    )
    out_specs = (P("kz", "en", None, None, None, None), P("kz", "en", None, None, None, None))
    return jax.shard_map(
        on_device, mesh=mesh, in_specs=in_specs, out_specs=out_specs, check_vma=False
    )
```

```python
import jax
import jax.numpy as jnp
from jax import lax
from jax.sharding import PartitionSpec as P
from jax.experimental import pallas as pl

OFFMAX = 4


DAMPING = 0.3


def padded(block, sides, width):
    for axis, dim in sides:
        count = lax.axis_size(axis)
        forward = [(i, i + 1) for i in range(count - 1)]
        backward = [(target, source) for source, target in forward]
        low = lax.ppermute(
            lax.slice_in_dim(block, block.shape[dim] - width, None, axis=dim), axis, forward
        )
        high = lax.ppermute(lax.slice_in_dim(block, 0, width, axis=dim), axis, backward)
        block = jnp.concatenate([low, block, high], axis=dim)
    return block


def matmul_high(left_matrix, right_matrix):
    return jnp.matmul(left_matrix, right_matrix, precision=lax.Precision.HIGHEST)


def complex_product(left_pair, right_pair):
    orbitals = left_pair[0].shape[-1]
    rows = jnp.concatenate([left_pair[0], left_pair[1]], axis=-2)
    cols = jnp.concatenate([right_pair[0], right_pair[1]], axis=-1)
    full = matmul_high(rows, cols)
    real_part = full[..., :orbitals, :orbitals] - full[..., orbitals:, orbitals:]
    imag_part = full[..., :orbitals, orbitals:] + full[..., orbitals:, :orbitals]
    return (real_part, imag_part)


def real_left(matrix, pair_value):
    orbitals = pair_value[0].shape[-1]
    full = matmul_high(matrix, jnp.concatenate([pair_value[0], pair_value[1]], axis=-1))
    return (full[..., :orbitals], full[..., orbitals:])


def real_right(pair_value, matrix):
    orbitals = pair_value[0].shape[-2]
    full = matmul_high(jnp.concatenate([pair_value[0], pair_value[1]], axis=-2), matrix)
    return (full[..., :orbitals, :], full[..., orbitals:, :])


def adjoint(pair_value):
    return (jnp.swapaxes(pair_value[0], -1, -2), -jnp.swapaxes(pair_value[1], -1, -2))


def add_pair(left_pair, right_pair):
    return (left_pair[0] + right_pair[0], left_pair[1] + right_pair[1])


def sub_pair(left_pair, right_pair):
    return (left_pair[0] - right_pair[0], left_pair[1] - right_pair[1])


def sweep_kernel(normal_re_ref, normal_im_ref, out_re_ref, out_im_ref):
    batch, orbitals, _ = normal_re_ref.shape
    out_re_ref[...] = normal_re_ref[...]
    out_im_ref[...] = normal_im_ref[...]
    lane = lax.broadcasted_iota(jnp.int32, (1, orbitals), 1)
    row_index = lax.broadcasted_iota(jnp.int32, (orbitals, 1), 0)

    def step(pivot, carry):
        lane_hit = lane == pivot
        row_hit = row_index == pivot
        for item in range(batch):
            whole_re = out_re_ref[item]
            whole_im = out_im_ref[item]
            row_re = out_re_ref[item, pl.ds(pivot, 1), :]
            row_im = out_im_ref[item, pl.ds(pivot, 1), :]
            col_re = jnp.sum(jnp.where(lane_hit, whole_re, 0.0), axis=1, keepdims=True)
            col_im = jnp.sum(jnp.where(lane_hit, whole_im, 0.0), axis=1, keepdims=True)
            piv_re = jnp.sum(jnp.where(lane_hit, row_re, 0.0), axis=1, keepdims=True)
            piv_im = jnp.sum(jnp.where(lane_hit, row_im, 0.0), axis=1, keepdims=True)
            norm = piv_re * piv_re + piv_im * piv_im
            inv_re = piv_re / norm
            inv_im = -piv_im / norm
            product_re = row_re * inv_re - row_im * inv_im
            product_im = row_re * inv_im + row_im * inv_re
            scaled_re = jnp.where(lane_hit, inv_re, product_re)
            scaled_im = jnp.where(lane_hit, inv_im, product_im)
            update_re = jnp.where(lane_hit, inv_re + 1.0, product_re)
            update_im = scaled_im
            col_re = jnp.where(row_hit, 0.0, col_re)
            col_im = jnp.where(row_hit, 0.0, col_im)
            out_re_ref[item] = whole_re - (col_re * update_re - col_im * update_im)
            out_im_ref[item] = whole_im - (col_re * update_im + col_im * update_re)
            out_re_ref[item, pl.ds(pivot, 1), :] = scaled_re
            out_im_ref[item, pl.ds(pivot, 1), :] = scaled_im
        return carry

    lax.fori_loop(0, orbitals, step, 0)


def hermitian_inverse(normal_pair, interpret=False):
    shape = normal_pair[0].shape
    orbitals = shape[-1]
    flat = [item.reshape(-1, orbitals, orbitals) for item in normal_pair]
    out_shape = jax.ShapeDtypeStruct(flat[0].shape, jnp.float32)
    inverse = pl.pallas_call(
        sweep_kernel,
        out_shape=(out_shape, out_shape),
        interpret=interpret,
    )(*flat)
    return (inverse[0].reshape(shape), inverse[1].reshape(shape))


def invert_pair(pair_value, interpret=False):
    adjoint_value = adjoint(pair_value)
    normal = complex_product(adjoint_value, pair_value)
    normal_inverse = hermitian_inverse(normal, interpret)
    return complex_product(normal_inverse, adjoint_value)


def greater_of(less_pair, ret_pair):
    return sub_pair(add_pair(less_pair, ret_pair), adjoint(ret_pair))


def pack_pair(pair_value):
    return jnp.stack([pair_value[0], pair_value[1]], axis=-3)


def green_blocks(sigma_less, sigma_great, hamilton, slab_coupling, energies):
    orbitals = sigma_less.shape[-1]
    slab_count = sigma_less.shape[2]
    identity = jnp.eye(orbitals, dtype=jnp.float32)
    energy_grid = energies[None, :, None, None]
    left_ret = []
    left_less = []
    for slab_index in range(slab_count):
        lesser = sigma_less[:, :, slab_index].astype(jnp.float32)
        greater = sigma_great[:, :, slab_index].astype(jnp.float32)
        retarded_re = 0.5 * (greater[:, :, 0] - lesser[:, :, 0])
        retarded_im = 0.5 * (greater[:, :, 1] - lesser[:, :, 1]) - DAMPING * identity
        system_re = energy_grid * identity - hamilton[:, :, slab_index] - retarded_re
        system_im = -retarded_im
        source = (lesser[:, :, 0], lesser[:, :, 1])
        if slab_index > 0:
            coupling = slab_coupling[slab_index - 1]
            folded = real_right(real_left(coupling, left_ret[-1]), coupling.T)
            system_re = system_re - folded[0]
            system_im = system_im - folded[1]
            source = add_pair(source, real_right(real_left(coupling, left_less[-1]), coupling.T))
        inverse = invert_pair((system_re, system_im))
        left_ret.append(inverse)
        left_less.append(complex_product(complex_product(inverse, source), adjoint(inverse)))
    full_ret = left_ret[-1]
    full_less = left_less[-1]
    lesser_list = [full_less]
    greater_list = [greater_of(full_less, full_ret)]
    for slab_index in range(slab_count - 2, -1, -1):
        coupling = slab_coupling[slab_index]
        green_couple = real_right(left_ret[slab_index], coupling)
        bridge = real_right(complex_product(green_couple, full_ret), coupling.T)
        cross_term = complex_product(bridge, left_less[slab_index])
        spread = complex_product(
            real_right(complex_product(green_couple, full_less), coupling.T),
            adjoint(left_ret[slab_index]),
        )
        full_less = add_pair(
            add_pair(left_less[slab_index], spread), sub_pair(cross_term, adjoint(cross_term))
        )
        full_ret = add_pair(left_ret[slab_index], complex_product(bridge, left_ret[slab_index]))
        lesser_list.insert(0, full_less)
        greater_list.insert(0, greater_of(full_less, full_ret))
    return [
        jnp.stack([pack_pair(less_item), pack_pair(great_item)], axis=2).astype(jnp.bfloat16)
        for less_item, great_item in zip(lesser_list, greater_list)
    ]


def hamiltonian(onsite_table, cos_coupling, slab_kind, momenta_index, momenta_total):
    kind_count = onsite_table.shape[0]
    choose = (slab_kind[:, None] == jnp.arange(kind_count, dtype=jnp.int32)[None, :]).astype(
        jnp.float32
    )
    onsite = jnp.einsum("sk,kij->sij", choose, onsite_table, precision=lax.Precision.HIGHEST)
    phase_factor = jnp.cos(2.0 * jnp.pi * momenta_index.astype(jnp.float32) / momenta_total)
    hamilton = onsite[None] + phase_factor[:, None, None, None] * cos_coupling[None]
    return hamilton[:, None]


def momentum_weights(table_rows, mode_weight, momenta_total):
    onehot = (
        table_rows[:, :, None] == jnp.arange(momenta_total, dtype=jnp.int32)[None, None, :]
    ).astype(jnp.float32)
    return (
        jnp.einsum("lq,aqk->lak", mode_weight, onehot, precision=lax.Precision.HIGHEST)
        / momenta_total
    )


def mixed_sums(extended, weights, form_factor, occupation, energy_offset, energy_count, margin):
    total_less = None
    total_great = None
    for mode_index in range(form_factor.shape[0]):
        shift_steps = energy_offset[mode_index]
        upper_side = lax.dynamic_slice_in_dim(extended, margin + shift_steps, energy_count, 1)
        lower_side = lax.dynamic_slice_in_dim(extended, margin - shift_steps, energy_count, 1)
        occupied = occupation[mode_index]
        less_term = (occupied + 1.0) * upper_side[:, :, 0].astype(
            jnp.float32
        ) + occupied * lower_side[:, :, 0].astype(jnp.float32)
        great_term = (occupied + 1.0) * lower_side[:, :, 1].astype(
            jnp.float32
        ) + occupied * upper_side[:, :, 1].astype(jnp.float32)
        mode_weights = weights[mode_index].reshape(
            weights.shape[1:] + (1,) * (less_term.ndim - 1)
        )
        less_sum = form_factor[mode_index] * jnp.sum(mode_weights * less_term[None], axis=1)
        great_sum = form_factor[mode_index] * jnp.sum(mode_weights * great_term[None], axis=1)
        total_less = less_sum if total_less is None else total_less + less_sum
        total_great = great_sum if total_great is None else total_great + great_sum
    return (total_less, total_great)


def exchange_blocks(blocks, width):
    count = lax.axis_size("kz")
    lanes = lax.axis_size("en")

    def far_of(index):
        return (index + 2) % count

    def joint(index, lane):
        return index * lanes + lane

    far = lax.ppermute(blocks, "kz", [(i, far_of(i)) for i in range(count)])
    tail = lax.slice_in_dim(blocks, blocks.shape[1] - width, None, axis=1)
    head = lax.slice_in_dim(blocks, 0, width, axis=1)
    forward = [(lane, lane + 1) for lane in range(lanes - 1)]
    backward = [(lane + 1, lane) for lane in range(lanes - 1)]
    low_same = lax.ppermute(tail, "en", forward)
    high_same = lax.ppermute(head, "en", backward)
    low_far = lax.ppermute(
        tail,
        ("kz", "en"),
        [(joint(far_of(i), lane), joint(i, lane + 1)) for i in range(count) for lane in range(lanes - 1)],
    )
    high_far = lax.ppermute(
        head,
        ("kz", "en"),
        [(joint(far_of(i), lane + 1), joint(i, lane)) for i in range(count) for lane in range(lanes - 1)],
    )
    own_extended = jnp.concatenate([low_same, blocks, high_same], axis=1)
    far_extended = jnp.concatenate([low_far, far, high_far], axis=1)
    return jnp.concatenate([own_extended, far_extended], axis=0)


def on_device(
    sigma_less,
    sigma_great,
    onsite_table,
    cos_coupling,
    slab_coupling,
    slab_kind,
    kz_table,
    mode_weight,
    form_factor,
    occupation,
    energy_offset,
):
    momenta_local = sigma_less.shape[0]
    energy_local = sigma_less.shape[1]
    momenta_total = momenta_local * lax.axis_size("kz")
    energy_total = energy_local * lax.axis_size("en")
    momenta_start = lax.axis_index("kz") * momenta_local
    momenta_index = momenta_start + jnp.arange(momenta_local, dtype=jnp.int32)
    energy_index = lax.axis_index("en") * energy_local + jnp.arange(energy_local, dtype=jnp.int32)
    energies = -1.5 + 3.0 * (energy_index.astype(jnp.float32) + 0.5) / energy_total
    hamilton = hamiltonian(onsite_table, cos_coupling, slab_kind, momenta_index, momenta_total)
    slab_blocks = green_blocks(sigma_less, sigma_great, hamilton, slab_coupling, energies)
    count = lax.axis_size("kz")
    momentum = lax.axis_index("kz")
    partner = momentum ^ 1
    held = jnp.stack([momentum, (momentum + 2) % count])
    all_weights = momentum_weights(kz_table, mode_weight, momenta_total)
    own_weights = jnp.take(jnp.take(all_weights, momentum[None], axis=1), held, axis=2)
    partner_weights = jnp.take(jnp.take(all_weights, partner[None], axis=1), held, axis=2)
    near_pairs = [(i, i ^ 1) for i in range(count)]
    less_parts = []
    great_parts = []
    slab_total = len(slab_blocks)
    groups = [[0], list(range(1, slab_total))] if slab_total > 1 else [[0]]
    for group in groups:
        blocks = jnp.stack([slab_blocks[slab_index] for slab_index in group], axis=3)
        extended = exchange_blocks(blocks, OFFMAX)
        settings = (form_factor, occupation, energy_offset, energy_local, OFFMAX)
        own_less, own_great = mixed_sums(extended, own_weights, *settings)
        partner_less, partner_great = mixed_sums(extended, partner_weights, *settings)
        arrived = lax.ppermute(jnp.stack([partner_less, partner_great]), "kz", near_pairs)
        less_parts.append((own_less + arrived[0]).astype(jnp.bfloat16))
        great_parts.append((own_great + arrived[1]).astype(jnp.bfloat16))
    return (jnp.concatenate(less_parts, axis=2), jnp.concatenate(great_parts, axis=2))


def solution(mesh):
    in_specs = (
        P("kz", "en", None, None, None, None),
        P("kz", "en", None, None, None, None),
        P(),
        P(),
        P(),
        P(),
        P(),
        P(),
        P(),
        P(),
        P(),
    )
    out_specs = (P("kz", "en", None, None, None, None), P("kz", "en", None, None, None, None))
    return jax.shard_map(
        on_device, mesh=mesh, in_specs=in_specs, out_specs=out_specs, check_vma=False
    )
```

```python
import jax
import jax.numpy as jnp
from jax import lax
from jax.sharding import PartitionSpec as P
from jax.experimental import pallas as pl

OFFMAX = 4


DAMPING = 0.3


def padded(block, sides, width):
    for axis, dim in sides:
        count = lax.axis_size(axis)
        forward = [(i, i + 1) for i in range(count - 1)]
        backward = [(target, source) for source, target in forward]
        low = lax.ppermute(
            lax.slice_in_dim(block, block.shape[dim] - width, None, axis=dim), axis, forward
        )
        high = lax.ppermute(lax.slice_in_dim(block, 0, width, axis=dim), axis, backward)
        block = jnp.concatenate([low, block, high], axis=dim)
    return block


def matmul_high(left_matrix, right_matrix):
    return jnp.matmul(left_matrix, right_matrix, precision=lax.Precision.HIGHEST)


def complex_product(left_pair, right_pair):
    orbitals = left_pair[0].shape[-1]
    rows = jnp.concatenate([left_pair[0], left_pair[1]], axis=-2)
    cols = jnp.concatenate([right_pair[0], right_pair[1]], axis=-1)
    full = matmul_high(rows, cols)
    real_part = full[..., :orbitals, :orbitals] - full[..., orbitals:, orbitals:]
    imag_part = full[..., :orbitals, orbitals:] + full[..., orbitals:, :orbitals]
    return (real_part, imag_part)


def real_left(matrix, pair_value):
    orbitals = pair_value[0].shape[-1]
    full = matmul_high(matrix, jnp.concatenate([pair_value[0], pair_value[1]], axis=-1))
    return (full[..., :orbitals], full[..., orbitals:])


def real_right(pair_value, matrix):
    orbitals = pair_value[0].shape[-2]
    full = matmul_high(jnp.concatenate([pair_value[0], pair_value[1]], axis=-2), matrix)
    return (full[..., :orbitals, :], full[..., orbitals:, :])


def split_pairs(full, count, axis):
    size = full.shape[axis] // (2 * count)
    pieces = [lax.slice_in_dim(full, i * size, (i + 1) * size, axis=axis) for i in range(2 * count)]
    return [(pieces[2 * i], pieces[2 * i + 1]) for i in range(count)]


def fold_many(matrix, pairs):
    flat = [part for pair in pairs for part in pair]
    left = matmul_high(matrix, jnp.concatenate(flat, axis=-1))
    full = matmul_high(jnp.concatenate(jnp.split(left, len(flat), axis=-1), axis=-2), matrix.T)
    return split_pairs(full, len(pairs), -2)


def products_shared_left(left_pair, right_pairs):
    orbitals = left_pair[0].shape[-1]
    rows = jnp.concatenate([left_pair[0], left_pair[1]], axis=-2)
    cols = jnp.concatenate([part for pair in right_pairs for part in pair], axis=-1)
    full = matmul_high(rows, cols)
    results = []
    for index in range(len(right_pairs)):
        start = 2 * index * orbitals
        top = full[..., :orbitals, :]
        bottom = full[..., orbitals:, :]
        real_part = top[..., start : start + orbitals] - bottom[..., start + orbitals : start + 2 * orbitals]
        imag_part = top[..., start + orbitals : start + 2 * orbitals] + bottom[..., start : start + orbitals]
        results.append((real_part, imag_part))
    return results


def real_right_many(pairs, matrix):
    flat = [part for pair in pairs for part in pair]
    full = matmul_high(jnp.concatenate(flat, axis=-2), matrix)
    return split_pairs(full, len(pairs), -2)


def adjoint(pair_value):
    return (jnp.swapaxes(pair_value[0], -1, -2), -jnp.swapaxes(pair_value[1], -1, -2))


def add_pair(left_pair, right_pair):
    return (left_pair[0] + right_pair[0], left_pair[1] + right_pair[1])


def sub_pair(left_pair, right_pair):
    return (left_pair[0] - right_pair[0], left_pair[1] - right_pair[1])


def sweep_kernel(normal_re_ref, normal_im_ref, out_re_ref, out_im_ref):
    batch, orbitals, _ = normal_re_ref.shape
    out_re_ref[...] = normal_re_ref[...]
    out_im_ref[...] = normal_im_ref[...]
    lane = lax.broadcasted_iota(jnp.int32, (1, orbitals), 1)
    row_index = lax.broadcasted_iota(jnp.int32, (orbitals, 1), 0)

    def step(pivot, carry):
        lane_hit = lane == pivot
        row_hit = row_index == pivot
        for item in range(batch):
            whole_re = out_re_ref[item]
            whole_im = out_im_ref[item]
            row_re = out_re_ref[item, pl.ds(pivot, 1), :]
            row_im = out_im_ref[item, pl.ds(pivot, 1), :]
            col_re = jnp.sum(jnp.where(lane_hit, whole_re, 0.0), axis=1, keepdims=True)
            col_im = jnp.sum(jnp.where(lane_hit, whole_im, 0.0), axis=1, keepdims=True)
            piv_re = jnp.sum(jnp.where(lane_hit, row_re, 0.0), axis=1, keepdims=True)
            piv_im = jnp.sum(jnp.where(lane_hit, row_im, 0.0), axis=1, keepdims=True)
            norm = piv_re * piv_re + piv_im * piv_im
            inv_re = piv_re / norm
            inv_im = -piv_im / norm
            product_re = row_re * inv_re - row_im * inv_im
            product_im = row_re * inv_im + row_im * inv_re
            scaled_re = jnp.where(lane_hit, inv_re, product_re)
            scaled_im = jnp.where(lane_hit, inv_im, product_im)
            update_re = jnp.where(lane_hit, inv_re + 1.0, product_re)
            update_im = scaled_im
            col_re = jnp.where(row_hit, 0.0, col_re)
            col_im = jnp.where(row_hit, 0.0, col_im)
            out_re_ref[item] = whole_re - (col_re * update_re - col_im * update_im)
            out_im_ref[item] = whole_im - (col_re * update_im + col_im * update_re)
            out_re_ref[item, pl.ds(pivot, 1), :] = scaled_re
            out_im_ref[item, pl.ds(pivot, 1), :] = scaled_im
        return carry

    lax.fori_loop(0, orbitals, step, 0)


def hermitian_inverse(normal_pair, interpret=False):
    shape = normal_pair[0].shape
    orbitals = shape[-1]
    flat = [item.reshape(-1, orbitals, orbitals) for item in normal_pair]
    out_shape = jax.ShapeDtypeStruct(flat[0].shape, jnp.float32)
    inverse = pl.pallas_call(
        sweep_kernel,
        out_shape=(out_shape, out_shape),
        interpret=interpret,
    )(*flat)
    return (inverse[0].reshape(shape), inverse[1].reshape(shape))


def invert_pair(pair_value, interpret=False):
    adjoint_value = adjoint(pair_value)
    normal = complex_product(adjoint_value, pair_value)
    normal_inverse = hermitian_inverse(normal, interpret)
    return complex_product(normal_inverse, adjoint_value)


def greater_of(less_pair, ret_pair):
    return sub_pair(add_pair(less_pair, ret_pair), adjoint(ret_pair))


def pack_pair(pair_value):
    return jnp.stack([pair_value[0], pair_value[1]], axis=-3)


def green_blocks(sigma_less, sigma_great, hamilton, slab_coupling, energies):
    orbitals = sigma_less.shape[-1]
    slab_count = sigma_less.shape[2]
    identity = jnp.eye(orbitals, dtype=jnp.float32)
    energy_grid = energies[None, :, None, None]
    left_ret = []
    left_less = []
    for slab_index in range(slab_count):
        lesser = sigma_less[:, :, slab_index].astype(jnp.float32)
        greater = sigma_great[:, :, slab_index].astype(jnp.float32)
        retarded_re = 0.5 * (greater[:, :, 0] - lesser[:, :, 0])
        retarded_im = 0.5 * (greater[:, :, 1] - lesser[:, :, 1]) - DAMPING * identity
        system_re = energy_grid * identity - hamilton[:, :, slab_index] - retarded_re
        system_im = -retarded_im
        source = (lesser[:, :, 0], lesser[:, :, 1])
        if slab_index > 0:
            coupling = slab_coupling[slab_index - 1]
            folded, folded_less = fold_many(coupling, [left_ret[-1], left_less[-1]])
            system_re = system_re - folded[0]
            system_im = system_im - folded[1]
            source = add_pair(source, folded_less)
        inverse = invert_pair((system_re, system_im))
        left_ret.append(inverse)
        left_less.append(complex_product(complex_product(inverse, source), adjoint(inverse)))
    full_ret = left_ret[-1]
    full_less = left_less[-1]
    lesser_list = [full_less]
    greater_list = [greater_of(full_less, full_ret)]
    for slab_index in range(slab_count - 2, -1, -1):
        coupling = slab_coupling[slab_index]
        green_couple = real_right(left_ret[slab_index], coupling)
        bridge, spread_left = real_right_many(
            products_shared_left(green_couple, [full_ret, full_less]), coupling.T
        )
        cross_term = complex_product(bridge, left_less[slab_index])
        spread = complex_product(spread_left, adjoint(left_ret[slab_index]))
        full_less = add_pair(
            add_pair(left_less[slab_index], spread), sub_pair(cross_term, adjoint(cross_term))
        )
        full_ret = add_pair(left_ret[slab_index], complex_product(bridge, left_ret[slab_index]))
        lesser_list.insert(0, full_less)
        greater_list.insert(0, greater_of(full_less, full_ret))
    return [
        jnp.stack([pack_pair(less_item), pack_pair(great_item)], axis=2).astype(jnp.bfloat16)
        for less_item, great_item in zip(lesser_list, greater_list)
    ]


def hamiltonian(onsite_table, cos_coupling, slab_kind, momenta_index, momenta_total):
    kind_count = onsite_table.shape[0]
    choose = (slab_kind[:, None] == jnp.arange(kind_count, dtype=jnp.int32)[None, :]).astype(
        jnp.float32
    )
    onsite = jnp.einsum("sk,kij->sij", choose, onsite_table, precision=lax.Precision.HIGHEST)
    phase_factor = jnp.cos(2.0 * jnp.pi * momenta_index.astype(jnp.float32) / momenta_total)
    hamilton = onsite[None] + phase_factor[:, None, None, None] * cos_coupling[None]
    return hamilton[:, None]


def momentum_weights(table_rows, mode_weight, momenta_total):
    onehot = (
        table_rows[:, :, None] == jnp.arange(momenta_total, dtype=jnp.int32)[None, None, :]
    ).astype(jnp.float32)
    return (
        jnp.einsum("lq,aqk->lak", mode_weight, onehot, precision=lax.Precision.HIGHEST)
        / momenta_total
    )


def mixed_sums(extended, weights, form_factor, occupation, energy_offset, energy_count, margin):
    total_less = None
    total_great = None
    for mode_index in range(form_factor.shape[0]):
        shift_steps = energy_offset[mode_index]
        upper_side = lax.dynamic_slice_in_dim(extended, margin + shift_steps, energy_count, 1)
        lower_side = lax.dynamic_slice_in_dim(extended, margin - shift_steps, energy_count, 1)
        occupied = occupation[mode_index]
        less_term = (occupied + 1.0) * upper_side[:, :, 0].astype(
            jnp.float32
        ) + occupied * lower_side[:, :, 0].astype(jnp.float32)
        great_term = (occupied + 1.0) * lower_side[:, :, 1].astype(
            jnp.float32
        ) + occupied * upper_side[:, :, 1].astype(jnp.float32)
        mode_weights = weights[mode_index].reshape(
            weights.shape[1:] + (1,) * (less_term.ndim - 1)
        )
        less_sum = form_factor[mode_index] * jnp.sum(mode_weights * less_term[None], axis=1)
        great_sum = form_factor[mode_index] * jnp.sum(mode_weights * great_term[None], axis=1)
        total_less = less_sum if total_less is None else total_less + less_sum
        total_great = great_sum if total_great is None else total_great + great_sum
    return (total_less, total_great)


def exchange_blocks(blocks, width):
    count = lax.axis_size("kz")
    lanes = lax.axis_size("en")

    def far_of(index):
        return (index + 2) % count

    def joint(index, lane):
        return index * lanes + lane

    far = lax.ppermute(blocks, "kz", [(i, far_of(i)) for i in range(count)])
    tail = lax.slice_in_dim(blocks, blocks.shape[1] - width, None, axis=1)
    head = lax.slice_in_dim(blocks, 0, width, axis=1)
    forward = [(lane, lane + 1) for lane in range(lanes - 1)]
    backward = [(lane + 1, lane) for lane in range(lanes - 1)]
    low_same = lax.ppermute(tail, "en", forward)
    high_same = lax.ppermute(head, "en", backward)
    low_far = lax.ppermute(
        tail,
        ("kz", "en"),
        [(joint(far_of(i), lane), joint(i, lane + 1)) for i in range(count) for lane in range(lanes - 1)],
    )
    high_far = lax.ppermute(
        head,
        ("kz", "en"),
        [(joint(far_of(i), lane + 1), joint(i, lane)) for i in range(count) for lane in range(lanes - 1)],
    )
    own_extended = jnp.concatenate([low_same, blocks, high_same], axis=1)
    far_extended = jnp.concatenate([low_far, far, high_far], axis=1)
    return jnp.concatenate([own_extended, far_extended], axis=0)


def on_device(
    sigma_less,
    sigma_great,
    onsite_table,
    cos_coupling,
    slab_coupling,
    slab_kind,
    kz_table,
    mode_weight,
    form_factor,
    occupation,
    energy_offset,
):
    momenta_local = sigma_less.shape[0]
    energy_local = sigma_less.shape[1]
    momenta_total = momenta_local * lax.axis_size("kz")
    energy_total = energy_local * lax.axis_size("en")
    momenta_start = lax.axis_index("kz") * momenta_local
    momenta_index = momenta_start + jnp.arange(momenta_local, dtype=jnp.int32)
    energy_index = lax.axis_index("en") * energy_local + jnp.arange(energy_local, dtype=jnp.int32)
    energies = -1.5 + 3.0 * (energy_index.astype(jnp.float32) + 0.5) / energy_total
    hamilton = hamiltonian(onsite_table, cos_coupling, slab_kind, momenta_index, momenta_total)
    slab_blocks = green_blocks(sigma_less, sigma_great, hamilton, slab_coupling, energies)
    count = lax.axis_size("kz")
    momentum = lax.axis_index("kz")
    partner = momentum ^ 1
    held = jnp.stack([momentum, (momentum + 2) % count])
    all_weights = momentum_weights(kz_table, mode_weight, momenta_total)
    own_weights = jnp.take(jnp.take(all_weights, momentum[None], axis=1), held, axis=2)
    partner_weights = jnp.take(jnp.take(all_weights, partner[None], axis=1), held, axis=2)
    near_pairs = [(i, i ^ 1) for i in range(count)]
    less_parts = []
    great_parts = []
    slab_total = len(slab_blocks)
    groups = [[0], list(range(1, slab_total))] if slab_total > 1 else [[0]]
    for group in groups:
        blocks = jnp.stack([slab_blocks[slab_index] for slab_index in group], axis=3)
        extended = exchange_blocks(blocks, OFFMAX)
        settings = (form_factor, occupation, energy_offset, energy_local, OFFMAX)
        own_less, own_great = mixed_sums(extended, own_weights, *settings)
        partner_less, partner_great = mixed_sums(extended, partner_weights, *settings)
        arrived = lax.ppermute(jnp.stack([partner_less, partner_great]), "kz", near_pairs)
        less_parts.append((own_less + arrived[0]).astype(jnp.bfloat16))
        great_parts.append((own_great + arrived[1]).astype(jnp.bfloat16))
    return (jnp.concatenate(less_parts, axis=2), jnp.concatenate(great_parts, axis=2))


def solution(mesh):
    in_specs = (
        P("kz", "en", None, None, None, None),
        P("kz", "en", None, None, None, None),
        P(),
        P(),
        P(),
        P(),
        P(),
        P(),
        P(),
        P(),
        P(),
    )
    out_specs = (P("kz", "en", None, None, None, None), P("kz", "en", None, None, None, None))
    return jax.shard_map(
        on_device, mesh=mesh, in_specs=in_specs, out_specs=out_specs, check_vma=False
    )
```

```python
import jax
import jax.numpy as jnp
from jax import lax
from jax.sharding import PartitionSpec as P
from jax.experimental import pallas as pl

OFFMAX = 4


DAMPING = 0.3


def padded(block, sides, width):
    for axis, dim in sides:
        count = lax.axis_size(axis)
        forward = [(i, i + 1) for i in range(count - 1)]
        backward = [(target, source) for source, target in forward]
        low = lax.ppermute(
            lax.slice_in_dim(block, block.shape[dim] - width, None, axis=dim), axis, forward
        )
        high = lax.ppermute(lax.slice_in_dim(block, 0, width, axis=dim), axis, backward)
        block = jnp.concatenate([low, block, high], axis=dim)
    return block


def matmul_high(left_matrix, right_matrix):
    return jnp.matmul(left_matrix, right_matrix, precision=lax.Precision.HIGHEST)


def complex_product(left_pair, right_pair):
    orbitals = left_pair[0].shape[-1]
    rows = jnp.concatenate([left_pair[0], left_pair[1]], axis=-2)
    cols = jnp.concatenate([right_pair[0], right_pair[1]], axis=-1)
    full = matmul_high(rows, cols)
    real_part = full[..., :orbitals, :orbitals] - full[..., orbitals:, orbitals:]
    imag_part = full[..., :orbitals, orbitals:] + full[..., orbitals:, :orbitals]
    return (real_part, imag_part)


def real_left(matrix, pair_value):
    orbitals = pair_value[0].shape[-1]
    full = matmul_high(matrix, jnp.concatenate([pair_value[0], pair_value[1]], axis=-1))
    return (full[..., :orbitals], full[..., orbitals:])


def real_right(pair_value, matrix):
    orbitals = pair_value[0].shape[-2]
    full = matmul_high(jnp.concatenate([pair_value[0], pair_value[1]], axis=-2), matrix)
    return (full[..., :orbitals, :], full[..., orbitals:, :])


def fold_many(matrix, pairs):
    flat = [part for pair in pairs for part in pair]
    left = matmul_high(matrix, jnp.concatenate(flat, axis=-1))
    full = matmul_high(jnp.concatenate(jnp.split(left, len(flat), axis=-1), axis=-2), matrix.T)
    pieces = jnp.split(full, len(flat), axis=-2)
    return [(pieces[2 * i], pieces[2 * i + 1]) for i in range(len(pairs))]


def adjoint(pair_value):
    return (jnp.swapaxes(pair_value[0], -1, -2), -jnp.swapaxes(pair_value[1], -1, -2))


def add_pair(left_pair, right_pair):
    return (left_pair[0] + right_pair[0], left_pair[1] + right_pair[1])


def sub_pair(left_pair, right_pair):
    return (left_pair[0] - right_pair[0], left_pair[1] - right_pair[1])


def sweep_kernel(normal_re_ref, normal_im_ref, out_re_ref, out_im_ref):
    batch, orbitals, _ = normal_re_ref.shape
    out_re_ref[...] = normal_re_ref[...]
    out_im_ref[...] = normal_im_ref[...]
    lane = lax.broadcasted_iota(jnp.int32, (1, orbitals), 1)
    row_index = lax.broadcasted_iota(jnp.int32, (orbitals, 1), 0)

    def step(pivot, carry):
        lane_hit = lane == pivot
        row_hit = row_index == pivot
        for item in range(batch):
            whole_re = out_re_ref[item]
            whole_im = out_im_ref[item]
            row_re = out_re_ref[item, pl.ds(pivot, 1), :]
            row_im = out_im_ref[item, pl.ds(pivot, 1), :]
            col_re = jnp.sum(jnp.where(lane_hit, whole_re, 0.0), axis=1, keepdims=True)
            col_im = jnp.sum(jnp.where(lane_hit, whole_im, 0.0), axis=1, keepdims=True)
            piv_re = jnp.sum(jnp.where(lane_hit, row_re, 0.0), axis=1, keepdims=True)
            piv_im = jnp.sum(jnp.where(lane_hit, row_im, 0.0), axis=1, keepdims=True)
            norm = piv_re * piv_re + piv_im * piv_im
            inv_re = piv_re / norm
            inv_im = -piv_im / norm
            product_re = row_re * inv_re - row_im * inv_im
            product_im = row_re * inv_im + row_im * inv_re
            scaled_re = jnp.where(lane_hit, inv_re, product_re)
            scaled_im = jnp.where(lane_hit, inv_im, product_im)
            update_re = jnp.where(lane_hit, inv_re + 1.0, product_re)
            update_im = scaled_im
            col_re = jnp.where(row_hit, 0.0, col_re)
            col_im = jnp.where(row_hit, 0.0, col_im)
            out_re_ref[item] = whole_re - (col_re * update_re - col_im * update_im)
            out_im_ref[item] = whole_im - (col_re * update_im + col_im * update_re)
            out_re_ref[item, pl.ds(pivot, 1), :] = scaled_re
            out_im_ref[item, pl.ds(pivot, 1), :] = scaled_im
        return carry

    lax.fori_loop(0, orbitals, step, 0)


def hermitian_inverse(normal_pair, interpret=False):
    shape = normal_pair[0].shape
    orbitals = shape[-1]
    flat = [item.reshape(-1, orbitals, orbitals) for item in normal_pair]
    out_shape = jax.ShapeDtypeStruct(flat[0].shape, jnp.float32)
    inverse = pl.pallas_call(
        sweep_kernel,
        out_shape=(out_shape, out_shape),
        interpret=interpret,
    )(*flat)
    return (inverse[0].reshape(shape), inverse[1].reshape(shape))


def invert_pair(pair_value, interpret=False):
    adjoint_value = adjoint(pair_value)
    normal = complex_product(adjoint_value, pair_value)
    normal_inverse = hermitian_inverse(normal, interpret)
    return complex_product(normal_inverse, adjoint_value)


def greater_of(less_pair, ret_pair):
    return sub_pair(add_pair(less_pair, ret_pair), adjoint(ret_pair))


def pack_pair(pair_value):
    return jnp.stack([pair_value[0], pair_value[1]], axis=-3)


def green_blocks(sigma_less, sigma_great, hamilton, slab_coupling, energies):
    orbitals = sigma_less.shape[-1]
    slab_count = sigma_less.shape[2]
    identity = jnp.eye(orbitals, dtype=jnp.float32)
    energy_grid = energies[None, :, None, None]
    left_ret = []
    left_less = []
    for slab_index in range(slab_count):
        lesser = sigma_less[:, :, slab_index].astype(jnp.float32)
        greater = sigma_great[:, :, slab_index].astype(jnp.float32)
        retarded_re = 0.5 * (greater[:, :, 0] - lesser[:, :, 0])
        retarded_im = 0.5 * (greater[:, :, 1] - lesser[:, :, 1]) - DAMPING * identity
        system_re = energy_grid * identity - hamilton[:, :, slab_index] - retarded_re
        system_im = -retarded_im
        source = (lesser[:, :, 0], lesser[:, :, 1])
        if slab_index > 0:
            coupling = slab_coupling[slab_index - 1]
            folded, folded_less = fold_many(coupling, [left_ret[-1], left_less[-1]])
            system_re = system_re - folded[0]
            system_im = system_im - folded[1]
            source = add_pair(source, folded_less)
        inverse = invert_pair((system_re, system_im))
        left_ret.append(inverse)
        left_less.append(complex_product(complex_product(inverse, source), adjoint(inverse)))
    full_ret = left_ret[-1]
    full_less = left_less[-1]
    lesser_list = [full_less]
    greater_list = [greater_of(full_less, full_ret)]
    for slab_index in range(slab_count - 2, -1, -1):
        coupling = slab_coupling[slab_index]
        green_couple = real_right(left_ret[slab_index], coupling)
        bridge = real_right(complex_product(green_couple, full_ret), coupling.T)
        cross_term = complex_product(bridge, left_less[slab_index])
        spread = complex_product(
            real_right(complex_product(green_couple, full_less), coupling.T),
            adjoint(left_ret[slab_index]),
        )
        full_less = add_pair(
            add_pair(left_less[slab_index], spread), sub_pair(cross_term, adjoint(cross_term))
        )
        full_ret = add_pair(left_ret[slab_index], complex_product(bridge, left_ret[slab_index]))
        lesser_list.insert(0, full_less)
        greater_list.insert(0, greater_of(full_less, full_ret))
    return [
        jnp.stack([pack_pair(less_item), pack_pair(great_item)], axis=2).astype(jnp.bfloat16)
        for less_item, great_item in zip(lesser_list, greater_list)
    ]


def hamiltonian(onsite_table, cos_coupling, slab_kind, momenta_index, momenta_total):
    kind_count = onsite_table.shape[0]
    choose = (slab_kind[:, None] == jnp.arange(kind_count, dtype=jnp.int32)[None, :]).astype(
        jnp.float32
    )
    onsite = jnp.einsum("sk,kij->sij", choose, onsite_table, precision=lax.Precision.HIGHEST)
    phase_factor = jnp.cos(2.0 * jnp.pi * momenta_index.astype(jnp.float32) / momenta_total)
    hamilton = onsite[None] + phase_factor[:, None, None, None] * cos_coupling[None]
    return hamilton[:, None]


def momentum_weights(table_rows, mode_weight, momenta_total):
    onehot = (
        table_rows[:, :, None] == jnp.arange(momenta_total, dtype=jnp.int32)[None, None, :]
    ).astype(jnp.float32)
    return (
        jnp.einsum("lq,aqk->lak", mode_weight, onehot, precision=lax.Precision.HIGHEST)
        / momenta_total
    )


def mixed_sums(extended, weights, form_factor, occupation, energy_offset, energy_count, margin):
    total_less = None
    total_great = None
    for mode_index in range(form_factor.shape[0]):
        shift_steps = energy_offset[mode_index]
        upper_side = lax.dynamic_slice_in_dim(extended, margin + shift_steps, energy_count, 1)
        lower_side = lax.dynamic_slice_in_dim(extended, margin - shift_steps, energy_count, 1)
        occupied = occupation[mode_index]
        less_term = (occupied + 1.0) * upper_side[:, :, 0].astype(
            jnp.float32
        ) + occupied * lower_side[:, :, 0].astype(jnp.float32)
        great_term = (occupied + 1.0) * lower_side[:, :, 1].astype(
            jnp.float32
        ) + occupied * upper_side[:, :, 1].astype(jnp.float32)
        mode_weights = weights[mode_index].reshape(
            weights.shape[1:] + (1,) * (less_term.ndim - 1)
        )
        less_sum = form_factor[mode_index] * jnp.sum(mode_weights * less_term[None], axis=1)
        great_sum = form_factor[mode_index] * jnp.sum(mode_weights * great_term[None], axis=1)
        total_less = less_sum if total_less is None else total_less + less_sum
        total_great = great_sum if total_great is None else total_great + great_sum
    return (total_less, total_great)


def exchange_blocks(blocks, width):
    count = lax.axis_size("kz")
    lanes = lax.axis_size("en")

    def far_of(index):
        return (index + 2) % count

    def joint(index, lane):
        return index * lanes + lane

    far = lax.ppermute(blocks, "kz", [(i, far_of(i)) for i in range(count)])
    tail = lax.slice_in_dim(blocks, blocks.shape[1] - width, None, axis=1)
    head = lax.slice_in_dim(blocks, 0, width, axis=1)
    forward = [(lane, lane + 1) for lane in range(lanes - 1)]
    backward = [(lane + 1, lane) for lane in range(lanes - 1)]
    low_same = lax.ppermute(tail, "en", forward)
    high_same = lax.ppermute(head, "en", backward)
    low_far = lax.ppermute(
        tail,
        ("kz", "en"),
        [(joint(far_of(i), lane), joint(i, lane + 1)) for i in range(count) for lane in range(lanes - 1)],
    )
    high_far = lax.ppermute(
        head,
        ("kz", "en"),
        [(joint(far_of(i), lane + 1), joint(i, lane)) for i in range(count) for lane in range(lanes - 1)],
    )
    own_extended = jnp.concatenate([low_same, blocks, high_same], axis=1)
    far_extended = jnp.concatenate([low_far, far, high_far], axis=1)
    return jnp.concatenate([own_extended, far_extended], axis=0)


def on_device(
    sigma_less,
    sigma_great,
    onsite_table,
    cos_coupling,
    slab_coupling,
    slab_kind,
    kz_table,
    mode_weight,
    form_factor,
    occupation,
    energy_offset,
):
    momenta_local = sigma_less.shape[0]
    energy_local = sigma_less.shape[1]
    momenta_total = momenta_local * lax.axis_size("kz")
    energy_total = energy_local * lax.axis_size("en")
    momenta_start = lax.axis_index("kz") * momenta_local
    momenta_index = momenta_start + jnp.arange(momenta_local, dtype=jnp.int32)
    energy_index = lax.axis_index("en") * energy_local + jnp.arange(energy_local, dtype=jnp.int32)
    energies = -1.5 + 3.0 * (energy_index.astype(jnp.float32) + 0.5) / energy_total
    hamilton = hamiltonian(onsite_table, cos_coupling, slab_kind, momenta_index, momenta_total)
    slab_blocks = green_blocks(sigma_less, sigma_great, hamilton, slab_coupling, energies)
    count = lax.axis_size("kz")
    momentum = lax.axis_index("kz")
    partner = momentum ^ 1
    held = jnp.stack([momentum, (momentum + 2) % count])
    all_weights = momentum_weights(kz_table, mode_weight, momenta_total)
    own_weights = jnp.take(jnp.take(all_weights, momentum[None], axis=1), held, axis=2)
    partner_weights = jnp.take(jnp.take(all_weights, partner[None], axis=1), held, axis=2)
    near_pairs = [(i, i ^ 1) for i in range(count)]
    less_parts = []
    great_parts = []
    slab_total = len(slab_blocks)
    groups = [[0], list(range(1, slab_total))] if slab_total > 1 else [[0]]
    for group in groups:
        blocks = jnp.stack([slab_blocks[slab_index] for slab_index in group], axis=3)
        extended = exchange_blocks(blocks, OFFMAX)
        settings = (form_factor, occupation, energy_offset, energy_local, OFFMAX)
        own_less, own_great = mixed_sums(extended, own_weights, *settings)
        partner_less, partner_great = mixed_sums(extended, partner_weights, *settings)
        arrived = lax.ppermute(jnp.stack([partner_less, partner_great]), "kz", near_pairs)
        less_parts.append((own_less + arrived[0]).astype(jnp.bfloat16))
        great_parts.append((own_great + arrived[1]).astype(jnp.bfloat16))
    return (jnp.concatenate(less_parts, axis=2), jnp.concatenate(great_parts, axis=2))


def solution(mesh):
    in_specs = (
        P("kz", "en", None, None, None, None),
        P("kz", "en", None, None, None, None),
        P(),
        P(),
        P(),
        P(),
        P(),
        P(),
        P(),
        P(),
        P(),
    )
    out_specs = (P("kz", "en", None, None, None, None), P("kz", "en", None, None, None, None))
    return jax.shard_map(
        on_device, mesh=mesh, in_specs=in_specs, out_specs=out_specs, check_vma=False
    )
```

```python
import jax
import jax.numpy as jnp
from jax import lax
from jax.sharding import PartitionSpec as P
from jax.experimental import pallas as pl

OFFMAX = 4


DAMPING = 0.3


def padded(block, sides, width):
    for axis, dim in sides:
        count = lax.axis_size(axis)
        forward = [(i, i + 1) for i in range(count - 1)]
        backward = [(target, source) for source, target in forward]
        low = lax.ppermute(
            lax.slice_in_dim(block, block.shape[dim] - width, None, axis=dim), axis, forward
        )
        high = lax.ppermute(lax.slice_in_dim(block, 0, width, axis=dim), axis, backward)
        block = jnp.concatenate([low, block, high], axis=dim)
    return block


def matmul_high(left_matrix, right_matrix):
    return jnp.matmul(left_matrix, right_matrix, precision=lax.Precision.HIGHEST)


def complex_product(left_pair, right_pair):
    orbitals = left_pair[0].shape[-1]
    rows = jnp.concatenate([left_pair[0], left_pair[1]], axis=-2)
    cols = jnp.concatenate([right_pair[0], right_pair[1]], axis=-1)
    full = matmul_high(rows, cols)
    real_part = full[..., :orbitals, :orbitals] - full[..., orbitals:, orbitals:]
    imag_part = full[..., :orbitals, orbitals:] + full[..., orbitals:, :orbitals]
    return (real_part, imag_part)


def real_left(matrix, pair_value):
    orbitals = pair_value[0].shape[-1]
    full = matmul_high(matrix, jnp.concatenate([pair_value[0], pair_value[1]], axis=-1))
    return (full[..., :orbitals], full[..., orbitals:])


def real_right(pair_value, matrix):
    orbitals = pair_value[0].shape[-2]
    full = matmul_high(jnp.concatenate([pair_value[0], pair_value[1]], axis=-2), matrix)
    return (full[..., :orbitals, :], full[..., orbitals:, :])


def adjoint(pair_value):
    return (jnp.swapaxes(pair_value[0], -1, -2), -jnp.swapaxes(pair_value[1], -1, -2))


def add_pair(left_pair, right_pair):
    return (left_pair[0] + right_pair[0], left_pair[1] + right_pair[1])


def sub_pair(left_pair, right_pair):
    return (left_pair[0] - right_pair[0], left_pair[1] - right_pair[1])


def sweep_kernel(normal_re_ref, normal_im_ref, out_re_ref, out_im_ref):
    batch, orbitals, _ = normal_re_ref.shape
    out_re_ref[...] = normal_re_ref[...]
    out_im_ref[...] = normal_im_ref[...]
    lane = lax.broadcasted_iota(jnp.int32, (1, orbitals), 1)
    row_index = lax.broadcasted_iota(jnp.int32, (orbitals, 1), 0)

    def step(pivot, carry):
        lane_hit = lane == pivot
        row_hit = row_index == pivot
        for item in range(batch):
            whole_re = out_re_ref[item]
            whole_im = out_im_ref[item]
            row_re = out_re_ref[item, pl.ds(pivot, 1), :]
            row_im = out_im_ref[item, pl.ds(pivot, 1), :]
            col_re = jnp.sum(jnp.where(lane_hit, whole_re, 0.0), axis=1, keepdims=True)
            col_im = jnp.sum(jnp.where(lane_hit, whole_im, 0.0), axis=1, keepdims=True)
            piv_re = jnp.sum(jnp.where(lane_hit, row_re, 0.0), axis=1, keepdims=True)
            piv_im = jnp.sum(jnp.where(lane_hit, row_im, 0.0), axis=1, keepdims=True)
            norm = piv_re * piv_re + piv_im * piv_im
            inv_re = piv_re / norm
            inv_im = -piv_im / norm
            product_re = row_re * inv_re - row_im * inv_im
            product_im = row_re * inv_im + row_im * inv_re
            scaled_re = jnp.where(lane_hit, inv_re, product_re)
            scaled_im = jnp.where(lane_hit, inv_im, product_im)
            update_re = jnp.where(lane_hit, inv_re + 1.0, product_re)
            update_im = scaled_im
            col_re = jnp.where(row_hit, 0.0, col_re)
            col_im = jnp.where(row_hit, 0.0, col_im)
            out_re_ref[item] = whole_re - (col_re * update_re - col_im * update_im)
            out_im_ref[item] = whole_im - (col_re * update_im + col_im * update_re)
            out_re_ref[item, pl.ds(pivot, 1), :] = scaled_re
            out_im_ref[item, pl.ds(pivot, 1), :] = scaled_im
        return carry

    lax.fori_loop(0, orbitals, step, 0)


def hermitian_inverse(normal_pair, interpret=False):
    shape = normal_pair[0].shape
    orbitals = shape[-1]
    flat = [item.reshape(-1, orbitals, orbitals) for item in normal_pair]
    out_shape = jax.ShapeDtypeStruct(flat[0].shape, jnp.float32)
    inverse = pl.pallas_call(
        sweep_kernel,
        out_shape=(out_shape, out_shape),
        interpret=interpret,
    )(*flat)
    return (inverse[0].reshape(shape), inverse[1].reshape(shape))


def invert_pair(pair_value, interpret=False):
    adjoint_value = adjoint(pair_value)
    normal = complex_product(adjoint_value, pair_value)
    normal_inverse = hermitian_inverse(normal, interpret)
    return complex_product(normal_inverse, adjoint_value)


def greater_of(less_pair, ret_pair):
    return sub_pair(add_pair(less_pair, ret_pair), adjoint(ret_pair))


def pack_pair(pair_value):
    return jnp.stack([pair_value[0], pair_value[1]], axis=-3)


def green_blocks(sigma_less, sigma_great, hamilton, slab_coupling, energies):
    orbitals = sigma_less.shape[-1]
    slab_count = sigma_less.shape[2]
    identity = jnp.eye(orbitals, dtype=jnp.float32)
    energy_grid = energies[None, :, None, None]
    left_ret = []
    left_less = []
    for slab_index in range(slab_count):
        lesser = sigma_less[:, :, slab_index].astype(jnp.float32)
        greater = sigma_great[:, :, slab_index].astype(jnp.float32)
        retarded_re = 0.5 * (greater[:, :, 0] - lesser[:, :, 0])
        retarded_im = 0.5 * (greater[:, :, 1] - lesser[:, :, 1]) - DAMPING * identity
        system_re = energy_grid * identity - hamilton[:, :, slab_index] - retarded_re
        system_im = -retarded_im
        source = (lesser[:, :, 0], lesser[:, :, 1])
        if slab_index > 0:
            coupling = slab_coupling[slab_index - 1]
            folded = real_right(real_left(coupling, left_ret[-1]), coupling.T)
            system_re = system_re - folded[0]
            system_im = system_im - folded[1]
            source = add_pair(source, real_right(real_left(coupling, left_less[-1]), coupling.T))
        inverse = invert_pair((system_re, system_im))
        left_ret.append(inverse)
        left_less.append(complex_product(complex_product(inverse, source), adjoint(inverse)))
    full_ret = left_ret[-1]
    full_less = left_less[-1]
    lesser_list = [full_less]
    greater_list = [greater_of(full_less, full_ret)]
    for slab_index in range(slab_count - 2, -1, -1):
        coupling = slab_coupling[slab_index]
        green_couple = real_right(left_ret[slab_index], coupling)
        bridge = real_right(complex_product(green_couple, full_ret), coupling.T)
        cross_term = complex_product(bridge, left_less[slab_index])
        spread = complex_product(
            real_right(complex_product(green_couple, full_less), coupling.T),
            adjoint(left_ret[slab_index]),
        )
        full_less = add_pair(
            add_pair(left_less[slab_index], spread), sub_pair(cross_term, adjoint(cross_term))
        )
        full_ret = add_pair(left_ret[slab_index], complex_product(bridge, left_ret[slab_index]))
        lesser_list.insert(0, full_less)
        greater_list.insert(0, greater_of(full_less, full_ret))
    return [
        jnp.stack([pack_pair(less_item), pack_pair(great_item)], axis=2).astype(jnp.bfloat16)
        for less_item, great_item in zip(lesser_list, greater_list)
    ]


def hamiltonian(onsite_table, cos_coupling, slab_kind, momenta_index, momenta_total):
    kind_count = onsite_table.shape[0]
    choose = (slab_kind[:, None] == jnp.arange(kind_count, dtype=jnp.int32)[None, :]).astype(
        jnp.float32
    )
    onsite = jnp.einsum("sk,kij->sij", choose, onsite_table, precision=lax.Precision.HIGHEST)
    phase_factor = jnp.cos(2.0 * jnp.pi * momenta_index.astype(jnp.float32) / momenta_total)
    hamilton = onsite[None] + phase_factor[:, None, None, None] * cos_coupling[None]
    return hamilton[:, None]


def momentum_weights(table_rows, mode_weight, momenta_total):
    onehot = (
        table_rows[:, :, None] == jnp.arange(momenta_total, dtype=jnp.int32)[None, None, :]
    ).astype(jnp.float32)
    return (
        jnp.einsum("lq,aqk->lak", mode_weight, onehot, precision=lax.Precision.HIGHEST)
        / momenta_total
    )


def mixed_sums(extended, weights, form_factor, occupation, energy_offset, energy_count, margin):
    total_less = None
    total_great = None
    for mode_index in range(form_factor.shape[0]):
        shift_steps = energy_offset[mode_index]
        upper_side = lax.dynamic_slice_in_dim(extended, margin + shift_steps, energy_count, 1)
        lower_side = lax.dynamic_slice_in_dim(extended, margin - shift_steps, energy_count, 1)
        occupied = occupation[mode_index]
        less_term = (occupied + 1.0) * upper_side[:, :, 0].astype(
            jnp.float32
        ) + occupied * lower_side[:, :, 0].astype(jnp.float32)
        great_term = (occupied + 1.0) * lower_side[:, :, 1].astype(
            jnp.float32
        ) + occupied * upper_side[:, :, 1].astype(jnp.float32)
        mode_weights = weights[mode_index].reshape(
            weights.shape[1:] + (1,) * (less_term.ndim - 1)
        )
        less_sum = form_factor[mode_index] * jnp.sum(mode_weights * less_term[None], axis=1)
        great_sum = form_factor[mode_index] * jnp.sum(mode_weights * great_term[None], axis=1)
        total_less = less_sum if total_less is None else total_less + less_sum
        total_great = great_sum if total_great is None else total_great + great_sum
    return (total_less, total_great)


def exchange_blocks(blocks, width):
    count = lax.axis_size("kz")
    lanes = lax.axis_size("en")

    def far_of(index):
        return (index + 2) % count

    def joint(index, lane):
        return index * lanes + lane

    far = lax.ppermute(blocks, "kz", [(i, far_of(i)) for i in range(count)])
    tail = lax.slice_in_dim(blocks, blocks.shape[1] - width, None, axis=1)
    head = lax.slice_in_dim(blocks, 0, width, axis=1)
    forward = [(lane, lane + 1) for lane in range(lanes - 1)]
    backward = [(lane + 1, lane) for lane in range(lanes - 1)]
    low_same = lax.ppermute(tail, "en", forward)
    high_same = lax.ppermute(head, "en", backward)
    low_far = lax.ppermute(
        tail,
        ("kz", "en"),
        [(joint(far_of(i), lane), joint(i, lane + 1)) for i in range(count) for lane in range(lanes - 1)],
    )
    high_far = lax.ppermute(
        head,
        ("kz", "en"),
        [(joint(far_of(i), lane + 1), joint(i, lane)) for i in range(count) for lane in range(lanes - 1)],
    )
    own_extended = jnp.concatenate([low_same, blocks, high_same], axis=1)
    far_extended = jnp.concatenate([low_far, far, high_far], axis=1)
    return jnp.concatenate([own_extended, far_extended], axis=0)


def on_device(
    sigma_less,
    sigma_great,
    onsite_table,
    cos_coupling,
    slab_coupling,
    slab_kind,
    kz_table,
    mode_weight,
    form_factor,
    occupation,
    energy_offset,
):
    momenta_local = sigma_less.shape[0]
    energy_local = sigma_less.shape[1]
    momenta_total = momenta_local * lax.axis_size("kz")
    energy_total = energy_local * lax.axis_size("en")
    momenta_start = lax.axis_index("kz") * momenta_local
    momenta_index = momenta_start + jnp.arange(momenta_local, dtype=jnp.int32)
    energy_index = lax.axis_index("en") * energy_local + jnp.arange(energy_local, dtype=jnp.int32)
    energies = -1.5 + 3.0 * (energy_index.astype(jnp.float32) + 0.5) / energy_total
    hamilton = hamiltonian(onsite_table, cos_coupling, slab_kind, momenta_index, momenta_total)
    slab_blocks = green_blocks(sigma_less, sigma_great, hamilton, slab_coupling, energies)
    count = lax.axis_size("kz")
    momentum = lax.axis_index("kz")
    partner = momentum ^ 1
    held = jnp.stack([momentum, (momentum + 2) % count])
    all_weights = momentum_weights(kz_table, mode_weight, momenta_total)
    own_weights = jnp.take(jnp.take(all_weights, momentum[None], axis=1), held, axis=2)
    partner_weights = jnp.take(jnp.take(all_weights, partner[None], axis=1), held, axis=2)
    both_weights = jnp.concatenate([own_weights, partner_weights], axis=1)
    near_pairs = [(i, i ^ 1) for i in range(count)]
    less_parts = []
    great_parts = []
    slab_total = len(slab_blocks)
    groups = [[0], list(range(1, slab_total))] if slab_total > 1 else [[0]]
    for group in groups:
        blocks = jnp.stack([slab_blocks[slab_index] for slab_index in group], axis=3)
        extended = exchange_blocks(blocks, OFFMAX)
        settings = (form_factor, occupation, energy_offset, energy_local, OFFMAX)
        both_less, both_great = mixed_sums(extended, both_weights, *settings)
        own_less, partner_less = both_less[:1], both_less[1:]
        own_great, partner_great = both_great[:1], both_great[1:]
        arrived = lax.ppermute(jnp.stack([partner_less, partner_great]), "kz", near_pairs)
        less_parts.append((own_less + arrived[0]).astype(jnp.bfloat16))
        great_parts.append((own_great + arrived[1]).astype(jnp.bfloat16))
    return (jnp.concatenate(less_parts, axis=2), jnp.concatenate(great_parts, axis=2))


def solution(mesh):
    in_specs = (
        P("kz", "en", None, None, None, None),
        P("kz", "en", None, None, None, None),
        P(),
        P(),
        P(),
        P(),
        P(),
        P(),
        P(),
        P(),
        P(),
    )
    out_specs = (P("kz", "en", None, None, None, None), P("kz", "en", None, None, None, None))
    return jax.shard_map(
        on_device, mesh=mesh, in_specs=in_specs, out_specs=out_specs, check_vma=False
    )
```
